128 devices in a mesh: seq: 32 (over x, y_lo, z), tp: 2 (over core), pd: 2 (over y_hi).
Axes of the slice: x: 4, y: 4 (y_hi: 2, y_lo: 2; y = y_hi * 2 + y_lo), z: 4, core: 2. Of those that a mesh axis runs over, the one named last changes fastest.
Arguments:
- hidden_in: bfloat16 [2, 8192, 2048], P('pd', 'seq'), may hold values from -6 to 6
- input_gain: float32 [2048], replicated, may hold values from 0.5 to 1.5
- w_query: bfloat16 [2048, 2048], P(None, 'tp'), may hold values from -0.125 to 0.125
- w_key: bfloat16 [2048, 256], P(None, 'tp'), may hold values from -0.125 to 0.125
- w_value: bfloat16 [2048, 256], P(None, 'tp'), may hold values from -0.125 to 0.125
- q_gain: float32 [128], replicated, may hold values from 0.1 to 1.9
- k_gain: float32 [128], replicated, may hold values from 0.1 to 1.9
- w_out: bfloat16 [2048, 2048], P('tp'), may hold values from -0.125 to 0.125
- post_gain: float32 [2048], replicated, may hold values from 0.5 to 1.5
- ctx_key: bfloat16 [2, 2048, 256], P('pd', 'seq', 'tp'), may hold values from -70 to 70
- ctx_value: bfloat16 [2, 2048, 256], P('pd', 'seq', 'tp'), may hold values from -6 to 6
- span_lens: int32 [2, 8], P('pd'), may hold values from 1 to 4096, 8192 in all within a row
- ctx_lens: int32 [2, 8], P('pd'), may hold values from 1 to 1024, 2048 in all within a row
- route_ids: int32 [2, 8192, 8], P('pd', ('seq', 'tp')), may hold values from 0 to 127, all different within a row; in each aligned block of 128 rows (0 to 127, 128 to 255, ..., all dimensions but the last counted through in order) at most 12 rows name the same one
- route_weights: float32 [2, 8192, 8], P('pd', ('seq', 'tp')), may hold values from 0.05 to 1
- w_gate_up: bfloat16 [128, 2048, 1536], P(('seq', 'tp', 'pd')), may hold values from -0.125 to 0.125
- w_down: bfloat16 [128, 768, 2048], P(('seq', 'tp', 'pd')), may hold values from -0.21875 to 0.21875
- earlier_kv: bfloat16 [8, 2, 8192, 2, 256], P(None, 'pd', 'seq', 'tp'), may hold values from -6 to 6
- page_table: int32 [8, 2, 64, 2], P(None, 'pd', 'seq', 'tp'), may hold values from 0 to 511, as said below
Outputs:
- layer_out: bfloat16 [2, 8192, 2048], P('pd', ('seq', 'tp'))
- decode_cache: bfloat16 [32, 2, 2, 16, 128, 256], P('seq', 'tp', 'pd')
The draws below stay inside these ranges and needn't reach their ends.
Inputs may be any that keep to these rules, and one draw needn't show every extreme that they name: `route_ids`: within the rows of one device no expert is named more than 12 times, a bound that some block reaches. `page_table`: an entry owner * 16 + slot sends the page to that slot of the device at index owner of seq, with the same indices of tp and pd. Every slot of every owner receives exactly one page; one device sends at most 1 pages to one owner, and exactly that many to some owner.
All inputs are finite; a program needn't handle non-finite values.
Results may differ from the reference program's by a relative error of at most 0.015.
Values may be sent and summed in bfloat16 or wider, within the bound.
No kernel may reach another device: no remote copies, remote signals or barrier semaphores. Data moves between devices by JAX's collectives and lax.ppermute only.
A program may use at most 128 MiB of HBM per device.

```python
import math
import jax
import jax.numpy as jnp
import numpy as np
from jax import lax

D = 2048
QH = 16
KVH = 2
HD = 128
FF = 768
TOP = 8
REQS = 8
PAGE = 128
LP = 8
TOK_DEV = 256
CTX_DEV = 64
SPAN = 8192
CTX = 2048
EXPERTS = 128
CAP = 12
PAGES_DEV = 16
N_SEQ = 32
N_TP = 2
N_PD = 2


def draw_ctx_key(key, part):
    shape = (N_PD, CTX_DEV * N_SEQ, KVH * HD)
    base = jax.random.truncated_normal(key, -6.0, 6.0, shape, jnp.float32)
    return base.astype(jnp.bfloat16)


def table_block(key):
    subkeys = jax.random.split(key, 3)
    source_order = jax.random.permutation(subkeys[0], N_SEQ)
    spread = max(PAGES_DEV, N_SEQ)
    offsets = jax.random.permutation(subkeys[1], spread)[:PAGES_DEV] % N_SEQ
    slot_orders = jax.vmap(lambda subkey: jax.random.permutation(subkey, PAGES_DEV))(jax.random.split(subkeys[2], N_SEQ))
    owners = (source_order[:, None] + offsets[None, :]) % N_SEQ
    slots = slot_orders[owners, jnp.arange(PAGES_DEV)[None, :]]
    values = owners * PAGES_DEV + slots
    per_device = TOK_DEV // PAGE
    values = values.reshape(N_SEQ, LP, per_device).transpose(1, 0, 2).reshape(LP, N_SEQ * per_device)
    return values


def draw_page_table(key, part):
    count = N_PD * KVH
    blocks = jax.vmap(table_block)(jax.random.split(jax.random.fold_in(key, 7), count))
    span_pages = N_SEQ * (TOK_DEV // PAGE)
    return blocks.reshape(N_PD, KVH, LP, span_pages).transpose(2, 0, 3, 1).astype(jnp.int32)


def shard_levels(key, dims, cuts, smallest, high):
    def one(position, parts):
        draws = jax.random.uniform(jax.random.fold_in(jax.random.fold_in(key, 6), position), (parts,), jnp.float32, smallest / len(cuts), high / len(cuts))
        return jnp.repeat(jnp.exp(draws), dims[position] // parts).reshape((-1,) + (1,) * (len(dims) - position - 1))

    factor_of = one(*cuts[0])
    for cut in cuts[1:]:
        factor_of = factor_of * one(*cut)
    return factor_of


def length_profile(count, total, bound, skew):
    loads = [(1 << 20) // math.isqrt(grade ** skew) + 1 for grade in range(2, count + 1)]
    rest, given = total - bound - (count - 1), [1] * (count - 1)
    while rest > 0:
        movable = [i for i in range(count - 1) if given[i] < bound]
        mass, remaining = sum([loads[i] for i in movable]), rest
        for i in movable:
            more = min(bound - given[i], max(1, remaining * loads[i] // mass), rest)
            given[i] = given[i] + more
            rest = rest - more
    return np.array([bound] + given)


def ragged_sizes(own_key, count, total, reach, lean):
    if count == 2:
        one = jax.random.randint(own_key, (), max(1, total - reach), min(reach, total - 1) + 1)
        return jnp.stack([one, total - one])
    tallies = jnp.asarray(length_profile(count, total, reach, lean), jnp.int32)
    couples = (count - 1) // 2
    donor, sink = tallies[1:1 + 2 * couples:2], tallies[2:2 + 2 * couples:2]
    slack = jnp.minimum(donor - 1, reach - sink)
    moved = jax.random.randint(jax.random.fold_in(own_key, 1), (couples,), 0, 1 << 20) % (slack + 1)
    tallies = tallies.at[1:1 + 2 * couples:2].set(donor - moved).at[2:2 + 2 * couples:2].set(sink + moved)
    return tallies[jax.random.permutation(jax.random.fold_in(own_key, 2), count)]


def routed_block(stream_key, own, number, rows, count, top, reach, skew):
    order = jax.random.permutation(stream_key, count)
    packed, common = portions_of(count, rows * top, reach, skew, True), portions_of(count, rows * top, reach, skew, False)
    places = jnp.arange(count)

    def named(sizes, turn):
        used = int((sizes > 0).sum())
        fixed = max(1, used // 4)
        moved = fixed + (places - fixed + turn * (used - fixed)) % max(1, count - fixed)
        return jnp.zeros((count,), jnp.int32).at[order[jnp.where(places < fixed, places, moved)]].set(jnp.asarray(sizes, jnp.int32))

    sizes = jnp.where(number % 4 == 0, named(packed, number // 4), named(common, number - number // 4 - 1))
    mixed = jax.random.permutation(jax.random.fold_in(own, 3), count)
    donor, sink = mixed[0:count // 2 * 2:2], mixed[1:count // 2 * 2:2]
    room = jnp.minimum(sizes[donor] - 1, reach - sizes[sink]) // 2
    room = jnp.where((donor == order[0]) | (sink == order[0]) | (sizes[sink] == 0), 0, jnp.maximum(room, 0))
    moved = jax.random.randint(jax.random.fold_in(own, 4), (count // 2,), 0, 1 << 20) % (room + 1)
    sizes = sizes.at[donor].add(-moved).at[sink].add(moved)
    labels = jnp.searchsorted(jnp.cumsum(sizes), jnp.arange(rows * top), side="right").astype(jnp.int32)
    grid = labels.reshape(top, rows).T
    grid = grid[jax.random.permutation(jax.random.fold_in(own, 1), rows)]
    turn = jax.random.randint(jax.random.fold_in(own, 2), (rows, 1), 0, top)
    return jnp.take_along_axis(grid, (jnp.arange(top)[None, :] + turn) % top, axis=1)


def portions_of(count, total, most, slope, full):
    portions = [(1 << 20) // math.isqrt(grade ** slope) + 1 for grade in range(1, count + 1)]
    largest = most if full else min(most, max(-(-total // count), total * portions[0] // sum(portions)))
    least = 1 if total - largest >= count - 1 else 0
    given, rest = [largest] + [least] * (count - 1), total - largest - least * (count - 1)
    while rest > 0:
        movable = [i for i in range(1, count) if given[i] < largest] or [i for i in range(1, count) if given[i] < most]
        pool, budget = sum([portions[i] for i in movable]), rest
        for i in movable:
            more = min(most - given[i], max(1, budget * portions[i] // pool), rest)
            given[i] = given[i] + more
            rest = rest - more
    return np.array(given)


def gaussian(own_key, dims, scale, reach, cuts=(), held_as=jnp.bfloat16):
    loudness = shard_levels(own_key, dims, cuts, -0.22, 0.18) if cuts else 1.0
    values = jax.random.normal(own_key, dims, jnp.float32) * scale * loudness
    return jnp.minimum(jnp.maximum(values, -reach), reach).astype(held_as)


def setup_inputs(seed: int = 0) -> dict:
    key_list = jax.random.split(jax.random.key(seed), 20)
    hidden_in = gaussian(key_list[0], (N_PD, SPAN, D), 1.0, 6.0, ((0, 2), (1, 32)))
    input_gain = jnp.clip(1.0 + 0.1 * jax.random.normal(key_list[1], (D,), jnp.float32), 0.5, 1.5)
    w_query = gaussian(key_list[2], (D, QH * HD), D ** -0.5, 0.125, ((1, 2),))
    w_key = gaussian(key_list[3], (D, KVH * HD), D ** -0.5, 0.125, ((1, 2),))
    w_value = gaussian(key_list[4], (D, KVH * HD), D ** -0.5, 0.125, ((1, 2),))
    q_gain = jnp.clip(1.0 + 0.18 * jax.random.normal(key_list[5], (HD,), jnp.float32), 0.1, 1.9)
    k_gain = jnp.clip(1.0 + 0.18 * jax.random.normal(key_list[6], (HD,), jnp.float32), 0.1, 1.9)
    w_out = gaussian(key_list[7], (QH * HD, D), (QH * HD) ** -0.5, 0.125, ((0, 2),))
    post_gain = jnp.clip(1.0 + 0.1 * jax.random.normal(key_list[8], (D,), jnp.float32), 0.5, 1.5)
    ctx_key = draw_ctx_key(jax.random.fold_in(key_list[19], 71), 0)
    ctx_value = gaussian(key_list[10], (N_PD, CTX, KVH * HD), 1.0, 6.0, ((0, 2), (1, 32), (2, 2)))
    span_lens = jax.vmap(lambda own: ragged_sizes(own, REQS, TOK_DEV * N_SEQ, TOK_DEV * N_SEQ // 2, 2))(jax.random.split(key_list[11], N_PD)).reshape((N_PD, REQS)).astype(jnp.int32)
    ctx_lens = jax.vmap(lambda own: ragged_sizes(own, REQS, CTX_DEV * N_SEQ, CTX_DEV * N_SEQ // 2, 2))(jax.random.split(key_list[12], N_PD)).reshape((N_PD, REQS)).astype(jnp.int32)
    route_ids_keys = jax.random.split(jax.random.fold_in(key_list[13], 1), N_PD * SPAN // (TOK_DEV // N_TP))
    route_ids_turns = jax.random.permutation(jax.random.fold_in(key_list[13], 3), N_PD * SPAN // (TOK_DEV // N_TP))
    route_ids = jax.vmap(lambda own, number: routed_block(jax.random.fold_in(key_list[13], 2), own, number, TOK_DEV // N_TP, EXPERTS, TOP, CAP, 2))(route_ids_keys, route_ids_turns).reshape((N_PD, SPAN, TOP))
    route_weights = jnp.clip(jnp.exp(math.log(1.0) - 2.9957323 * jax.random.uniform(key_list[14], (N_PD, SPAN, TOP), jnp.float32) ** shard_levels(key_list[14], (N_PD, SPAN, TOP), ((0, 2), (1, 64)), -0.2, 0.2)), 0.05, 1.0)
    w_gate_up = gaussian(key_list[15], (EXPERTS, D, 2 * FF), D ** -0.5, 0.125, ((0, 128),))
    w_down = gaussian(key_list[16], (EXPERTS, FF, D), FF ** -0.5, 0.21875, ((0, 128),))
    earlier_kv = gaussian(key_list[17], (LP, N_PD, SPAN, KVH, 2 * HD), 1.0, 6.0, ((1, 2), (2, 32), (3, 2)))
    page_table = draw_page_table(jax.random.fold_in(key_list[19], 71), 0)
    return {"hidden_in": hidden_in, "input_gain": input_gain, "w_query": w_query, "w_key": w_key, "w_value": w_value, "q_gain": q_gain, "k_gain": k_gain, "w_out": w_out, "post_gain": post_gain, "ctx_key": ctx_key, "ctx_value": ctx_value, "span_lens": span_lens, "ctx_lens": ctx_lens, "route_ids": route_ids, "route_weights": route_weights, "w_gate_up": w_gate_up, "w_down": w_down, "earlier_kv": earlier_kv, "page_table": page_table}


def rms_norm(values, gain):
    return values * lax.rsqrt(lax.optimization_barrier(jnp.mean(values * values, axis=-1, keepdims=True)) + 1e-06) * gain

def rotate(values, places):
    half = values.shape[-1] // 2
    freq = jnp.exp(jnp.arange(half, dtype=jnp.float32) * (-2.0 * math.log(1000000.0) / values.shape[-1]))
    angle = places.astype(jnp.float32)[:, None] * freq[None, :]
    cosine = jnp.cos(angle)[:, None, :]
    sine = jnp.sin(angle)[:, None, :]
    first = values[..., :half]
    second = values[..., half:]
    return jnp.concatenate([first * cosine - second * sine, second * cosine + first * sine], axis=-1)

def query_places(lengths, context_lengths, places):
    ends = jnp.cumsum(lengths).astype(jnp.int32)
    starts = ends - lengths
    request = lax.optimization_barrier(jnp.sum((places[:, None] >= ends[None, :]).astype(jnp.int32), axis=1)).astype(jnp.int32)
    member = request[:, None] == jnp.arange(lengths.shape[0], dtype=jnp.int32)[None, :]
    first = lax.optimization_barrier(jnp.sum(jnp.where(member, starts[None, :], 0), axis=1)).astype(jnp.int32)
    prior = lax.optimization_barrier(jnp.sum(jnp.where(member, context_lengths[None, :], 0), axis=1)).astype(jnp.int32)
    return (request, (places - first + prior).astype(jnp.int32))

def context_places(context_lengths, places):
    ends = jnp.cumsum(context_lengths).astype(jnp.int32)
    starts = ends - context_lengths
    request = lax.optimization_barrier(jnp.sum((places[:, None] >= ends[None, :]).astype(jnp.int32), axis=1)).astype(jnp.int32)
    member = request[:, None] == jnp.arange(context_lengths.shape[0], dtype=jnp.int32)[None, :]
    first = lax.optimization_barrier(jnp.sum(jnp.where(member, starts[None, :], 0), axis=1)).astype(jnp.int32)
    return (request, (places - first).astype(jnp.int32))

def group_attention(tokens, input_gain, w_query, w_key, w_value, q_gain, k_gain, w_out, post_gain, context_keys, context_values, lengths, context_lengths):
    span_places = jnp.arange(SPAN, dtype=jnp.int32)
    query_req, query_pos = query_places(lengths, context_lengths, span_places)
    ctx_req, ctx_pos = context_places(context_lengths, jnp.arange(CTX, dtype=jnp.int32))
    normed = rms_norm(tokens.astype(jnp.float32), input_gain).astype(jnp.bfloat16)
    query = jnp.dot(normed, w_query, preferred_element_type=jnp.float32).reshape(SPAN, QH, HD)
    key_proj = jnp.dot(normed, w_key, preferred_element_type=jnp.float32).reshape(SPAN, KVH, HD)
    value_proj = jnp.dot(normed, w_value, preferred_element_type=jnp.float32).astype(jnp.bfloat16)
    queries = rotate(rms_norm(query, q_gain), query_pos).astype(jnp.bfloat16)
    span_keys = rotate(rms_norm(key_proj, k_gain), query_pos).astype(jnp.bfloat16)
    all_keys = jnp.concatenate([context_keys.reshape(CTX, KVH, HD), span_keys], axis=0).astype(jnp.float32)
    all_values = jnp.concatenate([context_values.reshape(CTX, KVH, HD), value_proj.reshape(SPAN, KVH, HD)], axis=0).astype(jnp.float32)
    key_req = jnp.concatenate([ctx_req, query_req], axis=0)
    key_pos = jnp.concatenate([ctx_pos, query_pos], axis=0)
    group = QH // KVH
    block_rows = math.gcd(512, SPAN)
    count = SPAN // block_rows
    scale = 1.0 / math.sqrt(HD)

    def attend(items):
        query_block, req_block, pos_block = items
        scores = jnp.einsum('qhgd,khd->hgqk', query_block.astype(jnp.float32), all_keys) * scale
        visible = (req_block[:, None] == key_req[None, :]) & (key_pos[None, :] <= pos_block[:, None])
        scores = jnp.where(visible[None, None], scores, -jnp.inf)
        largest = lax.optimization_barrier(jnp.max(scores, axis=-1, keepdims=True))
        expo = jnp.exp(scores - largest)
        total = lax.optimization_barrier(jnp.sum(expo, axis=-1))
        probs = lax.optimization_barrier(expo.astype(jnp.bfloat16)).astype(jnp.float32)
        numer = jnp.einsum('hgqk,khd->hgqd', probs, all_values)
        result = numer / total[..., None]
        return result.transpose(2, 0, 1, 3).reshape(block_rows, QH * HD).astype(jnp.bfloat16)
    attn = lax.map(attend, (queries.reshape(count, block_rows, KVH, group, HD), query_req.reshape(count, block_rows), query_pos.reshape(count, block_rows)))
    attn = attn.reshape(SPAN, QH * HD)
    proj = jnp.dot(attn, w_out, preferred_element_type=jnp.float32)
    resid = (tokens.astype(jnp.float32) + proj).astype(jnp.bfloat16)
    mixed = rms_norm(resid.astype(jnp.float32), post_gain).astype(jnp.bfloat16)
    return (resid, mixed)

def reference(hidden_in, input_gain, w_query, w_key, w_value, q_gain, k_gain, w_out, post_gain, ctx_key, ctx_value, span_lens, ctx_lens, route_ids, route_weights, w_gate_up, w_down, earlier_kv, page_table):
    resid_parts = []
    mixed_parts = []
    for group_index in range(N_PD):
        resid, mixed = group_attention(hidden_in[group_index], input_gain, w_query, w_key, w_value, q_gain, k_gain, w_out, post_gain, ctx_key[group_index], ctx_value[group_index], span_lens[group_index], ctx_lens[group_index])
        resid_parts.append(resid)
        mixed_parts.append(mixed)
    resid_all = jnp.concatenate(resid_parts, axis=0)
    mixed_all = jnp.concatenate(mixed_parts, axis=0)
    row_ids = route_ids.reshape(-1).astype(jnp.int32)
    row_total = row_ids.shape[0]
    row_token = (jnp.arange(row_total, dtype=jnp.int32) // TOP).astype(jnp.int32)
    order = jnp.argsort(row_ids, stable=True).astype(jnp.int32)
    counts = lax.optimization_barrier(jnp.sum((row_ids[:, None] == jnp.arange(EXPERTS, dtype=jnp.int32)[None, :]).astype(jnp.int32), axis=0)).astype(jnp.int32)
    starts = (jnp.cumsum(counts) - counts).astype(jnp.int32)
    most_rows = N_SEQ * N_TP * N_PD * CAP
    padded = jnp.concatenate([order, jnp.zeros((most_rows,), jnp.int32)], axis=0)

    def expert(index):
        picked = lax.dynamic_slice(padded, (starts[index].astype(jnp.int32),), (most_rows,))
        rows = mixed_all[row_token[picked]]
        live = jnp.arange(most_rows, dtype=jnp.int32) < counts[index]
        hidden = jnp.dot(rows, w_gate_up[index], preferred_element_type=jnp.float32)
        act = (jax.nn.silu(hidden[:, :FF]) * hidden[:, FF:]).astype(jnp.bfloat16)
        out_rows = jnp.dot(act, w_down[index], preferred_element_type=jnp.float32).astype(jnp.bfloat16)
        return jnp.where(live[:, None], out_rows, jnp.zeros_like(out_rows))
    expert_rows = lax.map(expert, jnp.arange(EXPERTS, dtype=jnp.int32))
    inverse = jnp.zeros((row_total,), jnp.int32).at[order].set(jnp.arange(row_total, dtype=jnp.int32))
    within = (inverse - starts[row_ids]).astype(jnp.int32)
    gathered = expert_rows[row_ids, within]
    weights = route_weights.reshape(N_PD * SPAN, TOP)
    weights = weights / lax.optimization_barrier(jnp.sum(weights, axis=-1, keepdims=True))
    moe = jnp.einsum('tkd,tk->td', gathered.reshape(N_PD * SPAN, TOP, D).astype(jnp.float32), weights)
    layer_out = (resid_all.astype(jnp.float32) + moe).astype(jnp.bfloat16).reshape(N_PD, SPAN, D)
    span_pages = SPAN // PAGE
    pages = earlier_kv.reshape(LP, N_PD, span_pages, PAGE, KVH, 2 * HD).transpose(0, 1, 2, 4, 3, 5)
    owners = (page_table // PAGES_DEV).astype(jnp.int32)
    slots = (page_table % PAGES_DEV).astype(jnp.int32)
    group_index_all = lax.broadcasted_iota(jnp.int32, page_table.shape, 1)
    head_index_all = lax.broadcasted_iota(jnp.int32, page_table.shape, 3)
    decode_cache = jnp.zeros((N_SEQ, KVH, N_PD, PAGES_DEV, PAGE, 2 * HD), jnp.bfloat16)
    decode_cache = decode_cache.at[owners, head_index_all, group_index_all, slots].set(pages)
    return (layer_out, decode_cache)
```

```python
import math

import jax
import jax.numpy as jnp
from jax import lax
from jax.sharding import PartitionSpec as P

PAGE = 128


def rms_norm(values, gain):
    return values * lax.rsqrt(jnp.mean(values * values, axis=-1, keepdims=True) + 1e-06) * gain


def rotate(values, places):
    half = values.shape[-1] // 2
    freq = jnp.exp(
        jnp.arange(half, dtype=jnp.float32) * (-2.0 * math.log(1000000.0) / values.shape[-1])
    )
    angle = places.astype(jnp.float32)[:, None] * freq[None, :]
    cosine = jnp.cos(angle)[:, None, :]
    sine = jnp.sin(angle)[:, None, :]
    first = values[..., :half]
    second = values[..., half:]
    return jnp.concatenate(
        [first * cosine - second * sine, second * cosine + first * sine], axis=-1
    )


def query_places(lengths, context_lengths, places):
    ends = jnp.cumsum(lengths)
    starts = ends - lengths
    request = jnp.sum((places[:, None] >= ends[None, :]).astype(jnp.int32), axis=1)
    member = request[:, None] == jnp.arange(lengths.shape[0], dtype=jnp.int32)[None, :]
    first = jnp.sum(jnp.where(member, starts[None, :], 0), axis=1)
    prior = jnp.sum(jnp.where(member, context_lengths[None, :], 0), axis=1)
    return (request, places - first + prior)


def context_places(context_lengths, places):
    ends = jnp.cumsum(context_lengths)
    starts = ends - context_lengths
    request = jnp.sum((places[:, None] >= ends[None, :]).astype(jnp.int32), axis=1)
    member = request[:, None] == jnp.arange(context_lengths.shape[0], dtype=jnp.int32)[None, :]
    first = jnp.sum(jnp.where(member, starts[None, :], 0), axis=1)
    return (request, places - first)


def expert_mlp(arrived, w_gate_up, w_down):
    hidden = jnp.einsum("sejd,edf->sejf", arrived, w_gate_up, preferred_element_type=jnp.float32)
    inner = hidden.shape[-1] // 2
    act = (jax.nn.silu(hidden[..., :inner]) * hidden[..., inner:]).astype(jnp.bfloat16)
    return jnp.einsum("sejf,efd->sejd", act, w_down, preferred_element_type=jnp.float32).astype(
        jnp.bfloat16
    )


def shards(
    hidden_in,
    input_gain,
    w_query,
    w_key,
    w_value,
    q_gain,
    k_gain,
    w_out,
    post_gain,
    ctx_key,
    ctx_value,
    span_lens,
    ctx_lens,
    route_ids,
    route_weights,
    w_gate_up,
    w_down,
    earlier_kv,
    page_table,
):
    tokens = hidden_in[0]
    tok_count = tokens.shape[0]
    width = tokens.shape[1]
    ctx_count = ctx_key.shape[1]
    head_dim = q_gain.shape[0]
    seq_index = lax.axis_index("seq")
    span_places = seq_index * tok_count + jnp.arange(tok_count, dtype=jnp.int32)
    ctx_index = seq_index * ctx_count + jnp.arange(ctx_count, dtype=jnp.int32)
    query_req, query_pos = query_places(span_lens[0], ctx_lens[0], span_places)
    ctx_req, ctx_pos = context_places(ctx_lens[0], ctx_index)
    normed = rms_norm(tokens.astype(jnp.float32), input_gain).astype(jnp.bfloat16)
    query = jnp.dot(normed, w_query, preferred_element_type=jnp.float32)
    key_proj = jnp.dot(normed, w_key, preferred_element_type=jnp.float32)
    value_proj = jnp.dot(normed, w_value, preferred_element_type=jnp.float32).astype(jnp.bfloat16)
    query_heads = w_query.shape[1] // head_dim
    kv_local = w_key.shape[1] // head_dim
    group = query_heads // kv_local
    queries = rotate(
        rms_norm(query.reshape(tok_count, query_heads, head_dim), q_gain), query_pos
    ).astype(jnp.bfloat16)
    queries = queries.reshape(tok_count, kv_local, group, head_dim).transpose(1, 2, 0, 3)
    span_keys = rotate(
        rms_norm(key_proj.reshape(tok_count, kv_local, head_dim), k_gain), query_pos
    ).astype(jnp.bfloat16)
    all_keys = jnp.concatenate(
        [ctx_key[0], span_keys.reshape(tok_count, kv_local * head_dim)], axis=0
    )
    all_values = jnp.concatenate([ctx_value[0], value_proj], axis=0)
    seq_size = lax.axis_size("seq")
    every_ctx_req, every_ctx_pos = context_places(
        ctx_lens[0], jnp.arange(seq_size * ctx_count, dtype=jnp.int32)
    )
    every_query_req, every_query_pos = query_places(
        span_lens[0], ctx_lens[0], jnp.arange(seq_size * tok_count, dtype=jnp.int32)
    )
    piece_req = jnp.concatenate(
        [every_ctx_req.reshape(seq_size, ctx_count), every_query_req.reshape(seq_size, tok_count)],
        axis=1,
    ).reshape(-1)
    piece_pos = jnp.concatenate(
        [every_ctx_pos.reshape(seq_size, ctx_count), every_query_pos.reshape(seq_size, tok_count)],
        axis=1,
    ).reshape(-1)
    scale = 1.0 / math.sqrt(head_dim)
    start_state = (
        jnp.full((kv_local, group, tok_count), -1e30, jnp.float32),
        jnp.zeros((kv_local, group, tok_count), jnp.float32),
        jnp.zeros((kv_local, group, tok_count, head_dim), jnp.float32),
    )
    state = start_state
    kv_width = kv_local * head_dim
    local_kv = jnp.concatenate([all_keys, all_values], axis=1)
    every_kv = lax.all_to_all(
        jnp.broadcast_to(local_kv[None], (seq_size,) + local_kv.shape),
        "seq",
        split_axis=0,
        concat_axis=0,
        tiled=True,
    )
    piece_keys = every_kv[:, :, :kv_width].reshape(-1, kv_width)
    piece_values = every_kv[:, :, kv_width:].reshape(-1, kv_width)
    length = piece_keys.shape[0]
    block = length
    for candidate in (2048, 1280, 1024, 640, 512):
        block = candidate
        break
    count = length // block

    def advance(running, items):
        block_keys, block_values, block_req, block_pos = items
        key_heads = block_keys.reshape(block, kv_local, head_dim)
        value_heads = block_values.reshape(block, kv_local, head_dim)
        visible = (query_req[:, None] == block_req[None, :]) & (
            block_pos[None, :] <= query_pos[:, None]
        )
        largest, total, accum = running
        scores = (
            jnp.einsum("hgtd,khd->hgtk", queries, key_heads, preferred_element_type=jnp.float32)
            * scale
        )
        scores = jnp.where(visible[None, None], scores, -jnp.inf)
        new_largest = jnp.maximum(largest, jnp.max(scores, axis=-1))
        expo = jnp.exp(scores - new_largest[..., None])
        factor = jnp.exp(largest - new_largest)
        total = factor * total + jnp.sum(expo, axis=-1)
        accum = factor[..., None] * accum + jnp.einsum(
            "hgtk,khd->hgtd",
            expo.astype(jnp.bfloat16),
            value_heads,
            preferred_element_type=jnp.float32,
        )
        running = (new_largest, total, accum)
        return (running, None)

    stacked = (
        piece_keys.reshape(count, block, -1),
        piece_values.reshape(count, block, -1),
        piece_req.reshape(count, block),
        piece_pos.reshape(count, block),
    )
    state, _ = lax.scan(advance, state, stacked)
    largest, total, accum = state
    attn = (
        (accum / total[..., None])
        .transpose(2, 0, 1, 3)
        .reshape(tok_count, query_heads * head_dim)
        .astype(jnp.bfloat16)
    )
    half = tok_count // lax.axis_size("tp")
    proj = lax.psum_scatter(
        jnp.dot(attn, w_out, preferred_element_type=jnp.float32).astype(jnp.bfloat16),
        "tp",
        scatter_dimension=0,
        tiled=True,
    ).astype(jnp.float32)
    own_rows = lax.dynamic_slice_in_dim(tokens, lax.axis_index("tp") * half, half, 0)
    resid = (own_rows.astype(jnp.float32) + proj).astype(jnp.bfloat16)
    mixed = rms_norm(resid.astype(jnp.float32), post_gain).astype(jnp.bfloat16)
    top = route_ids.shape[2]
    row_ids = route_ids[0].reshape(-1)
    row_count = row_ids.shape[0]
    seq_tp = lax.axis_size("seq") * lax.axis_size("tp")
    pd_count = lax.axis_size("pd")
    device_count = seq_tp * pd_count
    exp_local = w_gate_up.shape[0]
    experts = device_count * exp_local
    capacity = max(2, 3 * tok_count * top // (2 * lax.axis_size("tp") * experts))
    picks = (row_ids[:, None] == jnp.arange(experts, dtype=jnp.int32)[None, :]).astype(jnp.bfloat16)
    earlier = (
        lax.broadcasted_iota(jnp.int32, (row_count, row_count), 0)
        > lax.broadcasted_iota(jnp.int32, (row_count, row_count), 1)
    ).astype(jnp.bfloat16)
    before = jnp.dot(earlier, picks, preferred_element_type=jnp.float32)
    rank = jnp.sum(before * picks.astype(jnp.float32), axis=1).astype(jnp.int32)
    target = row_ids * capacity + rank
    row_token = jnp.arange(row_count, dtype=jnp.int32) // top
    outgoing = jnp.zeros((experts * capacity, width), jnp.bfloat16).at[target].set(mixed[row_token])
    outgoing = outgoing.reshape(device_count, exp_local, capacity, width)
    returned = lax.all_to_all(
        expert_mlp(
            lax.all_to_all(outgoing, ("seq", "tp", "pd"), split_axis=0, concat_axis=0, tiled=True),
            w_gate_up,
            w_down,
        ),
        ("seq", "tp", "pd"),
        split_axis=0,
        concat_axis=0,
        tiled=True,
    )
    gathered = returned.reshape(experts * capacity, width)[target]
    weights = route_weights[0]
    weights = weights / jnp.sum(weights, axis=-1, keepdims=True)
    moe = jnp.einsum(
        "tkd,tk->td",
        gathered.reshape(half, top, width),
        weights,
        preferred_element_type=jnp.float32,
    )
    layer_out = (resid.astype(jnp.float32) + moe).astype(jnp.bfloat16)[None]
    layers = earlier_kv.shape[0]
    per_device = tok_count // PAGE
    page_count = layers * per_device
    page_cap = max(1, page_count // seq_size)
    pages = earlier_kv[:, 0].reshape(layers, per_device, PAGE, kv_local, 2 * head_dim)
    pages = pages.transpose(3, 0, 1, 2, 4).reshape(kv_local, page_count, PAGE, 2 * head_dim)
    table = page_table[:, 0].transpose(2, 0, 1).reshape(kv_local, page_count)
    owners = table // page_count
    slots = table % page_count
    order = jnp.arange(page_count, dtype=jnp.int32)
    same = (owners[:, :, None] == owners[:, None, :]) & (
        order[None, None, :] < order[None, :, None]
    )
    page_rank = jnp.sum(same.astype(jnp.int32), axis=2)
    page_target = owners * page_cap + page_rank
    head_rows = jnp.broadcast_to(jnp.arange(kv_local, dtype=jnp.int32)[:, None], page_target.shape)
    outgoing_pages = (
        jnp.zeros((kv_local, seq_size * page_cap, PAGE, 2 * head_dim), jnp.bfloat16)
        .at[head_rows, page_target]
        .set(pages)
    )
    outgoing_slots = (
        jnp.full((kv_local, seq_size * page_cap), -1, jnp.int32)
        .at[head_rows, page_target]
        .set(slots)
    )
    arrived_pages, arrived_slots = (
        lax.all_to_all(outgoing_pages, "seq", split_axis=1, concat_axis=1, tiled=True),
        lax.all_to_all(outgoing_slots, "seq", split_axis=1, concat_axis=1, tiled=True),
    )
    placing = (arrived_slots[:, None, :] == order[None, :, None]).astype(jnp.bfloat16)
    cache = jnp.einsum(
        "hkr,hrpc->hkpc", placing, arrived_pages, preferred_element_type=jnp.float32
    ).astype(jnp.bfloat16)
    decode_cache = cache[None, :, None]
    return (layer_out, decode_cache)


def solution(mesh):
    in_specs = (
        P("pd", "seq", None),
        P(),
        P(None, "tp"),
        P(None, "tp"),
        P(None, "tp"),
        P(),
        P(),
        P("tp", None),
        P(),
        P("pd", "seq", "tp"),
        P("pd", "seq", "tp"),
        P("pd", None),
        P("pd", None),
        P("pd", ("seq", "tp"), None),
        P("pd", ("seq", "tp"), None),
        P(("seq", "tp", "pd"), None, None),
        P(("seq", "tp", "pd"), None, None),
        P(None, "pd", "seq", "tp", None),
        P(None, "pd", "seq", "tp"),
    )
    out_specs = (P("pd", ("seq", "tp"), None), P("seq", "tp", "pd", None, None, None))
    return jax.shard_map(shards, mesh=mesh, in_specs=in_specs, out_specs=out_specs, check_vma=False)
```

```python
import functools
import math

import jax
import jax.numpy as jnp
from jax import lax
from jax.experimental import pallas as pl
from jax.experimental.pallas import tpu as pltpu
from jax.sharding import PartitionSpec as P

PAGE = 128


def rms_norm(values, gain):
    return values * lax.rsqrt(jnp.mean(values * values, axis=-1, keepdims=True) + 1e-06) * gain


def rotate(values, places):
    half = values.shape[-1] // 2
    freq = jnp.exp(
        jnp.arange(half, dtype=jnp.float32) * (-2.0 * math.log(1000000.0) / values.shape[-1])
    )
    angle = places.astype(jnp.float32)[:, None] * freq[None, :]
    cosine = jnp.cos(angle)[:, None, :]
    sine = jnp.sin(angle)[:, None, :]
    first = values[..., :half]
    second = values[..., half:]
    return jnp.concatenate(
        [first * cosine - second * sine, second * cosine + first * sine], axis=-1
    )


def query_places(lengths, context_lengths, places):
    ends = jnp.cumsum(lengths)
    starts = ends - lengths
    request = jnp.sum((places[:, None] >= ends[None, :]).astype(jnp.int32), axis=1)
    member = request[:, None] == jnp.arange(lengths.shape[0], dtype=jnp.int32)[None, :]
    first = jnp.sum(jnp.where(member, starts[None, :], 0), axis=1)
    prior = jnp.sum(jnp.where(member, context_lengths[None, :], 0), axis=1)
    return (request, places - first + prior)


def context_places(context_lengths, places):
    ends = jnp.cumsum(context_lengths)
    starts = ends - context_lengths
    request = jnp.sum((places[:, None] >= ends[None, :]).astype(jnp.int32), axis=1)
    member = request[:, None] == jnp.arange(context_lengths.shape[0], dtype=jnp.int32)[None, :]
    first = jnp.sum(jnp.where(member, starts[None, :], 0), axis=1)
    return (request, places - first)


KEY_BLOCK = 512


def flash_kernel(nkb, scale, live_ref, qreq_ref, qpos_ref, kreq_ref, kpos_ref, q_ref, k_ref, v_ref, o_ref, m_sc, l_sc, acc_sc):
    kb = pl.program_id(0)

    @pl.when(kb == 0)
    def _():
        m_sc[...] = jnp.full(m_sc.shape, -1e30, jnp.float32)
        l_sc[...] = jnp.zeros(l_sc.shape, jnp.float32)
        acc_sc[...] = jnp.zeros(acc_sc.shape, jnp.float32)

    @pl.when(live_ref[kb] > 0)
    def _():
        scores = lax.dot_general(
            q_ref[...], k_ref[...], (((1,), (1,)), ((), ())), preferred_element_type=jnp.float32
        ) * scale
        visible = (qreq_ref[...] == kreq_ref[...]) & (kpos_ref[...] <= qpos_ref[...])
        scores = jnp.where(visible, scores, -jnp.inf)
        m_old = m_sc[...]
        m_new = jnp.maximum(m_old, jnp.max(scores, axis=1, keepdims=True))
        expo = jnp.exp(scores - m_new)
        factor = jnp.exp(m_old - m_new)
        l_sc[...] = factor * l_sc[...] + jnp.sum(expo, axis=1, keepdims=True)
        acc_sc[...] = factor * acc_sc[...] + jnp.dot(
            expo.astype(jnp.bfloat16), v_ref[...], preferred_element_type=jnp.float32
        )
        m_sc[...] = m_new

    @pl.when(kb == nkb - 1)
    def _():
        o_ref[...] = (acc_sc[...] / l_sc[...]).astype(o_ref.dtype)


def flash_attention(live, qreq, qpos, kreq, kpos, q, k, v, scale):
    rows, head_dim = q.shape
    length = k.shape[0]
    nkb = length // KEY_BLOCK
    grid_spec = pltpu.PrefetchScalarGridSpec(
        num_scalar_prefetch=1,
        grid=(nkb,),
        in_specs=[
            pl.BlockSpec((rows, 1), lambda kb, live: (0, 0)),
            pl.BlockSpec((rows, 1), lambda kb, live: (0, 0)),
            pl.BlockSpec((1, KEY_BLOCK), lambda kb, live: (0, kb)),
            pl.BlockSpec((1, KEY_BLOCK), lambda kb, live: (0, kb)),
            pl.BlockSpec((rows, head_dim), lambda kb, live: (0, 0)),
            pl.BlockSpec((KEY_BLOCK, head_dim), lambda kb, live: (kb, 0)),
            pl.BlockSpec((KEY_BLOCK, head_dim), lambda kb, live: (kb, 0)),
        ],
        out_specs=pl.BlockSpec((rows, head_dim), lambda kb, live: (0, 0)),
        scratch_shapes=[
            pltpu.VMEM((rows, 1), jnp.float32),
            pltpu.VMEM((rows, 1), jnp.float32),
            pltpu.VMEM((rows, head_dim), jnp.float32),
        ],
    )
    flops = 4 * rows * length * head_dim
    return pl.pallas_call(
        functools.partial(flash_kernel, nkb, scale),
        grid_spec=grid_spec,
        out_shape=jax.ShapeDtypeStruct((rows, head_dim), jnp.bfloat16),
        compiler_params=pltpu.CompilerParams(dimension_semantics=("arbitrary",)),
        cost_estimate=pl.CostEstimate(
            flops=flops, transcendentals=rows * length, bytes_accessed=2 * length * head_dim * 2 + 2 * rows * head_dim * 2
        ),
    )(live, qreq, qpos, kreq, kpos, q, k, v)


def expert_mlp(arrived, w_gate_up, w_down):
    hidden = jnp.einsum("sejd,edf->sejf", arrived, w_gate_up, preferred_element_type=jnp.float32)
    inner = hidden.shape[-1] // 2
    act = (jax.nn.silu(hidden[..., :inner]) * hidden[..., inner:]).astype(jnp.bfloat16)
    return jnp.einsum("sejf,efd->sejd", act, w_down, preferred_element_type=jnp.float32).astype(
        jnp.bfloat16
    )


def shards(
    hidden_in,
    input_gain,
    w_query,
    w_key,
    w_value,
    q_gain,
    k_gain,
    w_out,
    post_gain,
    ctx_key,
    ctx_value,
    span_lens,
    ctx_lens,
    route_ids,
    route_weights,
    w_gate_up,
    w_down,
    earlier_kv,
    page_table,
):
    tokens = hidden_in[0]
    tok_count = tokens.shape[0]
    width = tokens.shape[1]
    ctx_count = ctx_key.shape[1]
    head_dim = q_gain.shape[0]
    seq_index = lax.axis_index("seq")
    span_places = seq_index * tok_count + jnp.arange(tok_count, dtype=jnp.int32)
    ctx_index = seq_index * ctx_count + jnp.arange(ctx_count, dtype=jnp.int32)
    query_req, query_pos = query_places(span_lens[0], ctx_lens[0], span_places)
    ctx_req, ctx_pos = context_places(ctx_lens[0], ctx_index)
    normed = rms_norm(tokens.astype(jnp.float32), input_gain).astype(jnp.bfloat16)
    query = jnp.dot(normed, w_query, preferred_element_type=jnp.float32)
    key_proj = jnp.dot(normed, w_key, preferred_element_type=jnp.float32)
    value_proj = jnp.dot(normed, w_value, preferred_element_type=jnp.float32).astype(jnp.bfloat16)
    query_heads = w_query.shape[1] // head_dim
    kv_local = w_key.shape[1] // head_dim
    group = query_heads // kv_local
    queries = rotate(
        rms_norm(query.reshape(tok_count, query_heads, head_dim), q_gain), query_pos
    ).astype(jnp.bfloat16)
    queries = queries.reshape(tok_count, kv_local, group, head_dim).transpose(1, 2, 0, 3)
    span_keys = rotate(
        rms_norm(key_proj.reshape(tok_count, kv_local, head_dim), k_gain), query_pos
    ).astype(jnp.bfloat16)
    all_keys = jnp.concatenate(
        [ctx_key[0], span_keys.reshape(tok_count, kv_local * head_dim)], axis=0
    )
    all_values = jnp.concatenate([ctx_value[0], value_proj], axis=0)
    seq_size = lax.axis_size("seq")
    every_ctx_req, every_ctx_pos = context_places(
        ctx_lens[0], jnp.arange(seq_size * ctx_count, dtype=jnp.int32)
    )
    every_query_req, every_query_pos = query_places(
        span_lens[0], ctx_lens[0], jnp.arange(seq_size * tok_count, dtype=jnp.int32)
    )
    key_req = jnp.concatenate([every_ctx_req, every_query_req], axis=0)
    key_pos = jnp.concatenate([every_ctx_pos, every_query_pos], axis=0)
    scale = 1.0 / math.sqrt(head_dim)
    kv_width = kv_local * head_dim
    local_kv = jnp.concatenate([all_keys, all_values], axis=1)
    every_kv = lax.all_to_all(
        jnp.broadcast_to(local_kv[None], (seq_size,) + local_kv.shape),
        "seq",
        split_axis=0,
        concat_axis=0,
        tiled=True,
    )
    ordered_kv = jnp.concatenate(
        [every_kv[:, :ctx_count].reshape(-1, 2 * kv_width), every_kv[:, ctx_count:].reshape(-1, 2 * kv_width)],
        axis=0,
    )
    length = ordered_kv.shape[0]
    seen = (query_req[:, None] == key_req[None, :]) & (key_pos[None, :] <= query_pos[:, None])
    live = jnp.any(jnp.any(seen, axis=0).reshape(length // KEY_BLOCK, KEY_BLOCK), axis=1).astype(jnp.int32)
    rows = group * tok_count
    qreq_rows = jnp.broadcast_to(query_req[None, :], (group, tok_count)).reshape(rows, 1)
    qpos_rows = jnp.broadcast_to(query_pos[None, :], (group, tok_count)).reshape(rows, 1)
    heads_out = []
    for h in range(kv_local):
        heads_out.append(
            flash_attention(
                live,
                qreq_rows,
                qpos_rows,
                key_req.reshape(1, length),
                key_pos.reshape(1, length),
                queries[h].reshape(rows, head_dim),
                ordered_kv[:, h * head_dim:(h + 1) * head_dim],
                ordered_kv[:, kv_width + h * head_dim:kv_width + (h + 1) * head_dim],
                scale,
            ).reshape(group, tok_count, head_dim)
        )
    attn = (
        jnp.stack(heads_out, axis=0)
        .transpose(2, 0, 1, 3)
        .reshape(tok_count, query_heads * head_dim)
    )
    half = tok_count // lax.axis_size("tp")
    proj = lax.psum_scatter(
        jnp.dot(attn, w_out, preferred_element_type=jnp.float32).astype(jnp.bfloat16),
        "tp",
        scatter_dimension=0,
        tiled=True,
    ).astype(jnp.float32)
    own_rows = lax.dynamic_slice_in_dim(tokens, lax.axis_index("tp") * half, half, 0)
    resid = (own_rows.astype(jnp.float32) + proj).astype(jnp.bfloat16)
    mixed = rms_norm(resid.astype(jnp.float32), post_gain).astype(jnp.bfloat16)
    top = route_ids.shape[2]
    row_ids = route_ids[0].reshape(-1)
    row_count = row_ids.shape[0]
    seq_tp = lax.axis_size("seq") * lax.axis_size("tp")
    pd_count = lax.axis_size("pd")
    device_count = seq_tp * pd_count
    exp_local = w_gate_up.shape[0]
    experts = device_count * exp_local
    capacity = max(2, 3 * tok_count * top // (2 * lax.axis_size("tp") * experts))
    picks = (row_ids[:, None] == jnp.arange(experts, dtype=jnp.int32)[None, :]).astype(jnp.bfloat16)
    earlier = (
        lax.broadcasted_iota(jnp.int32, (row_count, row_count), 0)
        > lax.broadcasted_iota(jnp.int32, (row_count, row_count), 1)
    ).astype(jnp.bfloat16)
    before = jnp.dot(earlier, picks, preferred_element_type=jnp.float32)
    rank = jnp.sum(before * picks.astype(jnp.float32), axis=1).astype(jnp.int32)
    target = row_ids * capacity + rank
    row_token = jnp.arange(row_count, dtype=jnp.int32) // top
    outgoing = jnp.zeros((experts * capacity, width), jnp.bfloat16).at[target].set(mixed[row_token])
    outgoing = outgoing.reshape(device_count, exp_local, capacity, width)
    returned = lax.all_to_all(
        expert_mlp(
            lax.all_to_all(outgoing, ("seq", "tp", "pd"), split_axis=0, concat_axis=0, tiled=True),
            w_gate_up,
            w_down,
        ),
        ("seq", "tp", "pd"),
        split_axis=0,
        concat_axis=0,
        tiled=True,
    )
    gathered = returned.reshape(experts * capacity, width)[target]
    weights = route_weights[0]
    weights = weights / jnp.sum(weights, axis=-1, keepdims=True)
    moe = jnp.einsum(
        "tkd,tk->td",
        gathered.reshape(half, top, width),
        weights,
        preferred_element_type=jnp.float32,
    )
    layer_out = (resid.astype(jnp.float32) + moe).astype(jnp.bfloat16)[None]
    layers = earlier_kv.shape[0]
    per_device = tok_count // PAGE
    page_count = layers * per_device
    page_cap = max(1, page_count // seq_size)
    pages = earlier_kv[:, 0].reshape(layers, per_device, PAGE, kv_local, 2 * head_dim)
    pages = pages.transpose(3, 0, 1, 2, 4).reshape(kv_local, page_count, PAGE, 2 * head_dim)
    table = page_table[:, 0].transpose(2, 0, 1).reshape(kv_local, page_count)
    owners = table // page_count
    slots = table % page_count
    order = jnp.arange(page_count, dtype=jnp.int32)
    same = (owners[:, :, None] == owners[:, None, :]) & (
        order[None, None, :] < order[None, :, None]
    )
    page_rank = jnp.sum(same.astype(jnp.int32), axis=2)
    page_target = owners * page_cap + page_rank
    head_rows = jnp.broadcast_to(jnp.arange(kv_local, dtype=jnp.int32)[:, None], page_target.shape)
    outgoing_pages = (
        jnp.zeros((kv_local, seq_size * page_cap, PAGE, 2 * head_dim), jnp.bfloat16)
        .at[head_rows, page_target]
        .set(pages)
    )
    outgoing_slots = (
        jnp.full((kv_local, seq_size * page_cap), -1, jnp.int32)
        .at[head_rows, page_target]
        .set(slots)
    )
    arrived_pages, arrived_slots = (
        lax.all_to_all(outgoing_pages, "seq", split_axis=1, concat_axis=1, tiled=True),
        lax.all_to_all(outgoing_slots, "seq", split_axis=1, concat_axis=1, tiled=True),
    )
    placing = (arrived_slots[:, None, :] == order[None, :, None]).astype(jnp.bfloat16)
    cache = jnp.einsum(
        "hkr,hrpc->hkpc", placing, arrived_pages, preferred_element_type=jnp.float32
    ).astype(jnp.bfloat16)
    decode_cache = cache[None, :, None]
    return (layer_out, decode_cache)


def solution(mesh):
    in_specs = (
        P("pd", "seq", None),
        P(),
        P(None, "tp"),
        P(None, "tp"),
        P(None, "tp"),
        P(),
        P(),
        P("tp", None),
        P(),
        P("pd", "seq", "tp"),
        P("pd", "seq", "tp"),
        P("pd", None),
        P("pd", None),
        P("pd", ("seq", "tp"), None),
        P("pd", ("seq", "tp"), None),
        P(("seq", "tp", "pd"), None, None),
        P(("seq", "tp", "pd"), None, None),
        P(None, "pd", "seq", "tp", None),
        P(None, "pd", "seq", "tp"),
    )
    out_specs = (P("pd", ("seq", "tp"), None), P("seq", "tp", "pd", None, None, None))
    return jax.shard_map(shards, mesh=mesh, in_specs=in_specs, out_specs=out_specs, check_vma=False)
```

```python
import functools
import math

import jax
import jax.numpy as jnp
from jax import lax
from jax.experimental import pallas as pl
from jax.experimental.pallas import tpu as pltpu
from jax.sharding import PartitionSpec as P

PAGE = 128


def rms_norm(values, gain):
    return values * lax.rsqrt(jnp.mean(values * values, axis=-1, keepdims=True) + 1e-06) * gain


def rotate(values, places):
    half = values.shape[-1] // 2
    freq = jnp.exp(
        jnp.arange(half, dtype=jnp.float32) * (-2.0 * math.log(1000000.0) / values.shape[-1])
    )
    angle = places.astype(jnp.float32)[:, None] * freq[None, :]
    cosine = jnp.cos(angle)[:, None, :]
    sine = jnp.sin(angle)[:, None, :]
    first = values[..., :half]
    second = values[..., half:]
    return jnp.concatenate(
        [first * cosine - second * sine, second * cosine + first * sine], axis=-1
    )


def query_places(lengths, context_lengths, places):
    ends = jnp.cumsum(lengths)
    starts = ends - lengths
    request = jnp.sum((places[:, None] >= ends[None, :]).astype(jnp.int32), axis=1)
    member = request[:, None] == jnp.arange(lengths.shape[0], dtype=jnp.int32)[None, :]
    first = jnp.sum(jnp.where(member, starts[None, :], 0), axis=1)
    prior = jnp.sum(jnp.where(member, context_lengths[None, :], 0), axis=1)
    return (request, places - first + prior)


def context_places(context_lengths, places):
    ends = jnp.cumsum(context_lengths)
    starts = ends - context_lengths
    request = jnp.sum((places[:, None] >= ends[None, :]).astype(jnp.int32), axis=1)
    member = request[:, None] == jnp.arange(context_lengths.shape[0], dtype=jnp.int32)[None, :]
    first = jnp.sum(jnp.where(member, starts[None, :], 0), axis=1)
    return (request, places - first)


KEY_BLOCK = 512


def flash_kernel(nkb, scale, live_ref, qreq_ref, qpos_ref, kreq_ref, kpos_ref, q_ref, k_ref, v_ref, o_ref, m_sc, l_sc, acc_sc):
    kb = pl.program_id(0)

    @pl.when(kb == 0)
    def _():
        m_sc[...] = jnp.full(m_sc.shape, -1e30, jnp.float32)
        l_sc[...] = jnp.zeros(l_sc.shape, jnp.float32)
        acc_sc[...] = jnp.zeros(acc_sc.shape, jnp.float32)

    @pl.when(live_ref[kb] > 0)
    def _():
        scores = lax.dot_general(
            q_ref[...], k_ref[...], (((1,), (1,)), ((), ())), preferred_element_type=jnp.float32
        ) * scale
        visible = (qreq_ref[...] == kreq_ref[...]) & (kpos_ref[...] <= qpos_ref[...])
        scores = jnp.where(visible, scores, -jnp.inf)
        m_old = m_sc[...]
        m_new = jnp.maximum(m_old, jnp.max(scores, axis=1, keepdims=True))
        expo = jnp.exp(scores - m_new)
        factor = jnp.exp(m_old - m_new)
        l_sc[...] = factor * l_sc[...] + jnp.sum(expo, axis=1, keepdims=True)
        acc_sc[...] = factor * acc_sc[...] + jnp.dot(
            expo.astype(jnp.bfloat16), v_ref[...], preferred_element_type=jnp.float32
        )
        m_sc[...] = m_new

    @pl.when(kb == nkb - 1)
    def _():
        o_ref[...] = (acc_sc[...] / l_sc[...]).astype(o_ref.dtype)


def flash_attention(live, qreq, qpos, kreq, kpos, q, k, v, scale):
    rows, head_dim = q.shape
    length = k.shape[0]
    nkb = length // KEY_BLOCK
    grid_spec = pltpu.PrefetchScalarGridSpec(
        num_scalar_prefetch=1,
        grid=(nkb,),
        in_specs=[
            pl.BlockSpec((rows, 1), lambda kb, live: (0, 0)),
            pl.BlockSpec((rows, 1), lambda kb, live: (0, 0)),
            pl.BlockSpec((1, KEY_BLOCK), lambda kb, live: (0, kb)),
            pl.BlockSpec((1, KEY_BLOCK), lambda kb, live: (0, kb)),
            pl.BlockSpec((rows, head_dim), lambda kb, live: (0, 0)),
            pl.BlockSpec((KEY_BLOCK, head_dim), lambda kb, live: (kb, 0)),
            pl.BlockSpec((KEY_BLOCK, head_dim), lambda kb, live: (kb, 0)),
        ],
        out_specs=pl.BlockSpec((rows, head_dim), lambda kb, live: (0, 0)),
        scratch_shapes=[
            pltpu.VMEM((rows, 1), jnp.float32),
            pltpu.VMEM((rows, 1), jnp.float32),
            pltpu.VMEM((rows, head_dim), jnp.float32),
        ],
    )
    flops = 4 * rows * length * head_dim
    return pl.pallas_call(
        functools.partial(flash_kernel, nkb, scale),
        grid_spec=grid_spec,
        out_shape=jax.ShapeDtypeStruct((rows, head_dim), jnp.bfloat16),
        compiler_params=pltpu.CompilerParams(dimension_semantics=("arbitrary",)),
        cost_estimate=pl.CostEstimate(
            flops=flops, transcendentals=rows * length, bytes_accessed=2 * length * head_dim * 2 + 2 * rows * head_dim * 2
        ),
    )(live, qreq, qpos, kreq, kpos, q, k, v)


def expert_mlp(arrived, w_gate_up, w_down):
    hidden = jnp.einsum("sejd,edf->sejf", arrived, w_gate_up, preferred_element_type=jnp.float32)
    inner = hidden.shape[-1] // 2
    act = (jax.nn.silu(hidden[..., :inner]) * hidden[..., inner:]).astype(jnp.bfloat16)
    return jnp.einsum("sejf,efd->sejd", act, w_down, preferred_element_type=jnp.float32).astype(
        jnp.bfloat16
    )


def shards(
    hidden_in,
    input_gain,
    w_query,
    w_key,
    w_value,
    q_gain,
    k_gain,
    w_out,
    post_gain,
    ctx_key,
    ctx_value,
    span_lens,
    ctx_lens,
    route_ids,
    route_weights,
    w_gate_up,
    w_down,
    earlier_kv,
    page_table,
):
    tokens = hidden_in[0]
    tok_count = tokens.shape[0]
    width = tokens.shape[1]
    ctx_count = ctx_key.shape[1]
    head_dim = q_gain.shape[0]
    seq_index = lax.axis_index("seq")
    span_places = seq_index * tok_count + jnp.arange(tok_count, dtype=jnp.int32)
    ctx_index = seq_index * ctx_count + jnp.arange(ctx_count, dtype=jnp.int32)
    query_req, query_pos = query_places(span_lens[0], ctx_lens[0], span_places)
    ctx_req, ctx_pos = context_places(ctx_lens[0], ctx_index)
    normed = rms_norm(tokens.astype(jnp.float32), input_gain).astype(jnp.bfloat16)
    query = jnp.dot(normed, w_query, preferred_element_type=jnp.float32)
    key_proj = jnp.dot(normed, w_key, preferred_element_type=jnp.float32)
    value_proj = jnp.dot(normed, w_value, preferred_element_type=jnp.float32).astype(jnp.bfloat16)
    query_heads = w_query.shape[1] // head_dim
    kv_local = w_key.shape[1] // head_dim
    group = query_heads // kv_local
    queries = rotate(
        rms_norm(query.reshape(tok_count, query_heads, head_dim), q_gain), query_pos
    ).astype(jnp.bfloat16)
    queries = queries.reshape(tok_count, kv_local, group, head_dim).transpose(1, 2, 0, 3)
    span_keys = rotate(
        rms_norm(key_proj.reshape(tok_count, kv_local, head_dim), k_gain), query_pos
    ).astype(jnp.bfloat16)
    all_keys = jnp.concatenate(
        [ctx_key[0], span_keys.reshape(tok_count, kv_local * head_dim)], axis=0
    )
    all_values = jnp.concatenate([ctx_value[0], value_proj], axis=0)
    seq_size = lax.axis_size("seq")
    every_ctx_req, every_ctx_pos = context_places(
        ctx_lens[0], jnp.arange(seq_size * ctx_count, dtype=jnp.int32)
    )
    every_query_req, every_query_pos = query_places(
        span_lens[0], ctx_lens[0], jnp.arange(seq_size * tok_count, dtype=jnp.int32)
    )
    key_req = jnp.concatenate([every_ctx_req, every_query_req], axis=0)
    key_pos = jnp.concatenate([every_ctx_pos, every_query_pos], axis=0)
    scale = 1.0 / math.sqrt(head_dim)
    kv_width = kv_local * head_dim
    local_kv = jnp.concatenate([all_keys, all_values], axis=1)
    every_kv = lax.all_to_all(
        jnp.broadcast_to(local_kv[None], (seq_size,) + local_kv.shape),
        "seq",
        split_axis=0,
        concat_axis=0,
        tiled=True,
    )
    ordered_kv = jnp.concatenate(
        [every_kv[:, :ctx_count].reshape(-1, 2 * kv_width), every_kv[:, ctx_count:].reshape(-1, 2 * kv_width)],
        axis=0,
    )
    length = ordered_kv.shape[0]
    seen = (query_req[:, None] == key_req[None, :]) & (key_pos[None, :] <= query_pos[:, None])
    live = jnp.any(jnp.any(seen, axis=0).reshape(length // KEY_BLOCK, KEY_BLOCK), axis=1).astype(jnp.int32)
    rows = group * tok_count
    qreq_rows = jnp.broadcast_to(query_req[None, :], (group, tok_count)).reshape(rows, 1)
    qpos_rows = jnp.broadcast_to(query_pos[None, :], (group, tok_count)).reshape(rows, 1)
    heads_out = []
    for h in range(kv_local):
        heads_out.append(
            flash_attention(
                live,
                qreq_rows,
                qpos_rows,
                key_req.reshape(1, length),
                key_pos.reshape(1, length),
                queries[h].reshape(rows, head_dim),
                ordered_kv[:, h * head_dim:(h + 1) * head_dim],
                ordered_kv[:, kv_width + h * head_dim:kv_width + (h + 1) * head_dim],
                scale,
            ).reshape(group, tok_count, head_dim)
        )
    attn = (
        jnp.stack(heads_out, axis=0)
        .transpose(2, 0, 1, 3)
        .reshape(tok_count, query_heads * head_dim)
    )
    half = tok_count // lax.axis_size("tp")
    proj = lax.psum_scatter(
        jnp.dot(attn, w_out, preferred_element_type=jnp.float32).astype(jnp.bfloat16),
        "tp",
        scatter_dimension=0,
        tiled=True,
    ).astype(jnp.float32)
    own_rows = lax.dynamic_slice_in_dim(tokens, lax.axis_index("tp") * half, half, 0)
    resid = (own_rows.astype(jnp.float32) + proj).astype(jnp.bfloat16)
    mixed = rms_norm(resid.astype(jnp.float32), post_gain).astype(jnp.bfloat16)
    top = route_ids.shape[2]
    row_ids = route_ids[0].reshape(-1)
    row_count = row_ids.shape[0]
    seq_tp = lax.axis_size("seq") * lax.axis_size("tp")
    pd_count = lax.axis_size("pd")
    device_count = seq_tp * pd_count
    exp_local = w_gate_up.shape[0]
    experts = device_count * exp_local
    capacity = max(2, 3 * tok_count * top // (2 * lax.axis_size("tp") * experts))
    picks = (row_ids[:, None] == jnp.arange(experts, dtype=jnp.int32)[None, :]).astype(jnp.bfloat16)
    earlier = (
        lax.broadcasted_iota(jnp.int32, (row_count, row_count), 0)
        > lax.broadcasted_iota(jnp.int32, (row_count, row_count), 1)
    ).astype(jnp.bfloat16)
    before = jnp.dot(earlier, picks, preferred_element_type=jnp.float32)
    rank = jnp.sum(before * picks.astype(jnp.float32), axis=1).astype(jnp.int32)
    target = row_ids * capacity + rank
    row_token = jnp.arange(row_count, dtype=jnp.int32) // top
    lanes = 128
    chunks = width // lanes
    moe_axes = ("seq", "tp", "pd")
    outgoing = (
        jnp.zeros((experts * capacity, chunks, lanes), jnp.bfloat16)
        .at[target]
        .set(mixed.reshape(half, chunks, lanes)[row_token])
    )
    outgoing = outgoing.reshape(device_count, exp_local * capacity * chunks, lanes)
    arrived = lax.all_to_all(outgoing, moe_axes, split_axis=0, concat_axis=0, tiled=True)
    done = expert_mlp(arrived.reshape(device_count, exp_local, capacity, width), w_gate_up, w_down)
    returned = lax.all_to_all(
        done.reshape(device_count, exp_local * capacity * chunks, lanes),
        moe_axes,
        split_axis=0,
        concat_axis=0,
        tiled=True,
    )
    gathered = returned.reshape(experts * capacity, chunks, lanes)[target]
    weights = route_weights[0]
    weights = weights / jnp.sum(weights, axis=-1, keepdims=True)
    moe = jnp.einsum(
        "tkcl,tk->tcl",
        gathered.reshape(half, top, chunks, lanes),
        weights,
        preferred_element_type=jnp.float32,
    ).reshape(half, width)
    layer_out = (resid.astype(jnp.float32) + moe).astype(jnp.bfloat16)[None]
    layers = earlier_kv.shape[0]
    per_device = tok_count // PAGE
    page_count = layers * per_device
    page_cap = max(1, page_count // seq_size)
    pages = earlier_kv[:, 0].reshape(layers, per_device, PAGE, kv_local, 2 * head_dim)
    pages = pages.transpose(3, 0, 1, 2, 4).reshape(kv_local, page_count, PAGE, 2 * head_dim)
    table = page_table[:, 0].transpose(2, 0, 1).reshape(kv_local, page_count)
    owners = table // page_count
    slots = table % page_count
    order = jnp.arange(page_count, dtype=jnp.int32)
    same = (owners[:, :, None] == owners[:, None, :]) & (
        order[None, None, :] < order[None, :, None]
    )
    page_rank = jnp.sum(same.astype(jnp.int32), axis=2)
    page_target = owners * page_cap + page_rank
    head_rows = jnp.broadcast_to(jnp.arange(kv_local, dtype=jnp.int32)[:, None], page_target.shape)
    outgoing_pages = (
        jnp.zeros((kv_local, seq_size * page_cap, PAGE, 2 * head_dim), jnp.bfloat16)
        .at[head_rows, page_target]
        .set(pages)
    )
    outgoing_slots = (
        jnp.full((kv_local, seq_size * page_cap), -1, jnp.int32)
        .at[head_rows, page_target]
        .set(slots)
    )
    arrived_pages, arrived_slots = (
        lax.all_to_all(outgoing_pages, "seq", split_axis=1, concat_axis=1, tiled=True),
        lax.all_to_all(outgoing_slots, "seq", split_axis=1, concat_axis=1, tiled=True),
    )
    placing = (arrived_slots[:, None, :] == order[None, :, None]).astype(jnp.bfloat16)
    cache = jnp.einsum(
        "hkr,hrpc->hkpc", placing, arrived_pages, preferred_element_type=jnp.float32
    ).astype(jnp.bfloat16)
    decode_cache = cache[None, :, None]
    return (layer_out, decode_cache)


def solution(mesh):
    in_specs = (
        P("pd", "seq", None),
        P(),
        P(None, "tp"),
        P(None, "tp"),
        P(None, "tp"),
        P(),
        P(),
        P("tp", None),
        P(),
        P("pd", "seq", "tp"),
        P("pd", "seq", "tp"),
        P("pd", None),
        P("pd", None),
        P("pd", ("seq", "tp"), None),
        P("pd", ("seq", "tp"), None),
        P(("seq", "tp", "pd"), None, None),
        P(("seq", "tp", "pd"), None, None),
        P(None, "pd", "seq", "tp", None),
        P(None, "pd", "seq", "tp"),
    )
    out_specs = (P("pd", ("seq", "tp"), None), P("seq", "tp", "pd", None, None, None))
    return jax.shard_map(shards, mesh=mesh, in_specs=in_specs, out_specs=out_specs, check_vma=False)
```

```python
import functools
import math

import jax
import jax.numpy as jnp
from jax import lax
from jax.experimental import pallas as pl
from jax.experimental.pallas import tpu as pltpu
from jax.sharding import PartitionSpec as P

PAGE = 128


def rms_norm(values, gain):
    return values * lax.rsqrt(jnp.mean(values * values, axis=-1, keepdims=True) + 1e-06) * gain


def rotate(values, places):
    half = values.shape[-1] // 2
    freq = jnp.exp(
        jnp.arange(half, dtype=jnp.float32) * (-2.0 * math.log(1000000.0) / values.shape[-1])
    )
    angle = places.astype(jnp.float32)[:, None] * freq[None, :]
    cosine = jnp.cos(angle)[:, None, :]
    sine = jnp.sin(angle)[:, None, :]
    first = values[..., :half]
    second = values[..., half:]
    return jnp.concatenate(
        [first * cosine - second * sine, second * cosine + first * sine], axis=-1
    )


def query_places(lengths, context_lengths, places):
    ends = jnp.cumsum(lengths)
    starts = ends - lengths
    request = jnp.sum((places[:, None] >= ends[None, :]).astype(jnp.int32), axis=1)
    member = request[:, None] == jnp.arange(lengths.shape[0], dtype=jnp.int32)[None, :]
    first = jnp.sum(jnp.where(member, starts[None, :], 0), axis=1)
    prior = jnp.sum(jnp.where(member, context_lengths[None, :], 0), axis=1)
    return (request, places - first + prior)


def context_places(context_lengths, places):
    ends = jnp.cumsum(context_lengths)
    starts = ends - context_lengths
    request = jnp.sum((places[:, None] >= ends[None, :]).astype(jnp.int32), axis=1)
    member = request[:, None] == jnp.arange(context_lengths.shape[0], dtype=jnp.int32)[None, :]
    first = jnp.sum(jnp.where(member, starts[None, :], 0), axis=1)
    return (request, places - first)


KEY_BLOCK = 512


def flash_kernel(nkb, scale, live_ref, qreq_ref, qpos_ref, kreq_ref, kpos_ref, q_ref, k_ref, v_ref, o_ref, m_sc, l_sc, acc_sc):
    kb = pl.program_id(0)

    @pl.when(kb == 0)
    def _():
        m_sc[...] = jnp.full(m_sc.shape, -1e30, jnp.float32)
        l_sc[...] = jnp.zeros(l_sc.shape, jnp.float32)
        acc_sc[...] = jnp.zeros(acc_sc.shape, jnp.float32)

    @pl.when(live_ref[kb] > 0)
    def _():
        scores = lax.dot_general(
            q_ref[...], k_ref[...], (((1,), (1,)), ((), ())), preferred_element_type=jnp.float32
        ) * scale
        visible = (qreq_ref[...] == kreq_ref[...]) & (kpos_ref[...] <= qpos_ref[...])
        scores = jnp.where(visible, scores, -jnp.inf)
        m_old = m_sc[...]
        m_new = jnp.maximum(m_old, jnp.max(scores, axis=1, keepdims=True))
        expo = jnp.exp(scores - m_new)
        factor = jnp.exp(m_old - m_new)
        l_sc[...] = factor * l_sc[...] + jnp.sum(expo, axis=1, keepdims=True)
        acc_sc[...] = factor * acc_sc[...] + jnp.dot(
            expo.astype(jnp.bfloat16), v_ref[...], preferred_element_type=jnp.float32
        )
        m_sc[...] = m_new

    @pl.when(kb == nkb - 1)
    def _():
        o_ref[...] = (acc_sc[...] / l_sc[...]).astype(o_ref.dtype)


def flash_attention(live, qreq, qpos, kreq, kpos, q, k, v, scale):
    rows, head_dim = q.shape
    length = k.shape[0]
    nkb = length // KEY_BLOCK
    grid_spec = pltpu.PrefetchScalarGridSpec(
        num_scalar_prefetch=1,
        grid=(nkb,),
        in_specs=[
            pl.BlockSpec((rows, 1), lambda kb, live: (0, 0)),
            pl.BlockSpec((rows, 1), lambda kb, live: (0, 0)),
            pl.BlockSpec((1, KEY_BLOCK), lambda kb, live: (0, kb)),
            pl.BlockSpec((1, KEY_BLOCK), lambda kb, live: (0, kb)),
            pl.BlockSpec((rows, head_dim), lambda kb, live: (0, 0)),
            pl.BlockSpec((KEY_BLOCK, head_dim), lambda kb, live: (kb, 0)),
            pl.BlockSpec((KEY_BLOCK, head_dim), lambda kb, live: (kb, 0)),
        ],
        out_specs=pl.BlockSpec((rows, head_dim), lambda kb, live: (0, 0)),
        scratch_shapes=[
            pltpu.VMEM((rows, 1), jnp.float32),
            pltpu.VMEM((rows, 1), jnp.float32),
            pltpu.VMEM((rows, head_dim), jnp.float32),
        ],
    )
    flops = 4 * rows * length * head_dim
    return pl.pallas_call(
        functools.partial(flash_kernel, nkb, scale),
        grid_spec=grid_spec,
        out_shape=jax.ShapeDtypeStruct((rows, head_dim), jnp.bfloat16),
        compiler_params=pltpu.CompilerParams(dimension_semantics=("arbitrary",)),
        cost_estimate=pl.CostEstimate(
            flops=flops, transcendentals=rows * length, bytes_accessed=2 * length * head_dim * 2 + 2 * rows * head_dim * 2
        ),
    )(live, qreq, qpos, kreq, kpos, q, k, v)


def expert_mlp(arrived, w_gate_up, w_down):
    hidden = jnp.einsum("sejd,edf->sejf", arrived, w_gate_up, preferred_element_type=jnp.float32)
    inner = hidden.shape[-1] // 2
    act = (jax.nn.silu(hidden[..., :inner]) * hidden[..., inner:]).astype(jnp.bfloat16)
    return jnp.einsum("sejf,efd->sejd", act, w_down, preferred_element_type=jnp.float32).astype(
        jnp.bfloat16
    )


def shards(
    hidden_in,
    input_gain,
    w_query,
    w_key,
    w_value,
    q_gain,
    k_gain,
    w_out,
    post_gain,
    ctx_key,
    ctx_value,
    span_lens,
    ctx_lens,
    route_ids,
    route_weights,
    w_gate_up,
    w_down,
    earlier_kv,
    page_table,
):
    tokens = hidden_in[0]
    tok_count = tokens.shape[0]
    width = tokens.shape[1]
    ctx_count = ctx_key.shape[1]
    head_dim = q_gain.shape[0]
    seq_index = lax.axis_index("seq")
    span_places = seq_index * tok_count + jnp.arange(tok_count, dtype=jnp.int32)
    ctx_index = seq_index * ctx_count + jnp.arange(ctx_count, dtype=jnp.int32)
    query_req, query_pos = query_places(span_lens[0], ctx_lens[0], span_places)
    ctx_req, ctx_pos = context_places(ctx_lens[0], ctx_index)
    normed = rms_norm(tokens.astype(jnp.float32), input_gain).astype(jnp.bfloat16)
    query = jnp.dot(normed, w_query, preferred_element_type=jnp.float32)
    key_proj = jnp.dot(normed, w_key, preferred_element_type=jnp.float32)
    value_proj = jnp.dot(normed, w_value, preferred_element_type=jnp.float32).astype(jnp.bfloat16)
    query_heads = w_query.shape[1] // head_dim
    kv_local = w_key.shape[1] // head_dim
    group = query_heads // kv_local
    queries = rotate(
        rms_norm(query.reshape(tok_count, query_heads, head_dim), q_gain), query_pos
    ).astype(jnp.bfloat16)
    queries = queries.reshape(tok_count, kv_local, group, head_dim).transpose(1, 2, 0, 3)
    span_keys = rotate(
        rms_norm(key_proj.reshape(tok_count, kv_local, head_dim), k_gain), query_pos
    ).astype(jnp.bfloat16)
    all_keys = jnp.concatenate(
        [ctx_key[0], span_keys.reshape(tok_count, kv_local * head_dim)], axis=0
    )
    all_values = jnp.concatenate([ctx_value[0], value_proj], axis=0)
    seq_size = lax.axis_size("seq")
    every_ctx_req, every_ctx_pos = context_places(
        ctx_lens[0], jnp.arange(seq_size * ctx_count, dtype=jnp.int32)
    )
    every_query_req, every_query_pos = query_places(
        span_lens[0], ctx_lens[0], jnp.arange(seq_size * tok_count, dtype=jnp.int32)
    )
    key_req = jnp.concatenate([every_ctx_req, every_query_req], axis=0)
    key_pos = jnp.concatenate([every_ctx_pos, every_query_pos], axis=0)
    scale = 1.0 / math.sqrt(head_dim)
    kv_width = kv_local * head_dim
    local_kv = jnp.concatenate([all_keys, all_values], axis=1)
    every_kv = lax.all_to_all(
        jnp.broadcast_to(local_kv[None], (seq_size,) + local_kv.shape),
        "seq",
        split_axis=0,
        concat_axis=0,
        tiled=True,
    )
    layers = earlier_kv.shape[0]
    per_device = tok_count // PAGE
    page_count = layers * per_device
    page_cap = max(1, page_count // seq_size)
    pages = earlier_kv[:, 0].reshape(layers, per_device, PAGE, kv_local, 2 * head_dim)
    pages = pages.transpose(3, 0, 1, 2, 4).reshape(kv_local, page_count, PAGE, 2 * head_dim)
    table = page_table[:, 0].transpose(2, 0, 1).reshape(kv_local, page_count)
    owners = table // page_count
    slots = table % page_count
    order = jnp.arange(page_count, dtype=jnp.int32)
    same = (owners[:, :, None] == owners[:, None, :]) & (
        order[None, None, :] < order[None, :, None]
    )
    page_rank = jnp.sum(same.astype(jnp.int32), axis=2)
    page_target = owners * page_cap + page_rank
    head_rows = jnp.broadcast_to(jnp.arange(kv_local, dtype=jnp.int32)[:, None], page_target.shape)
    outgoing_pages = (
        jnp.zeros((kv_local, seq_size * page_cap, PAGE, 2 * head_dim), jnp.bfloat16)
        .at[head_rows, page_target]
        .set(pages)
    )
    outgoing_pages, every_kv = lax.optimization_barrier((outgoing_pages, every_kv))
    outgoing_slots = (
        jnp.full((kv_local, seq_size * page_cap), -1, jnp.int32)
        .at[head_rows, page_target]
        .set(slots)
    )
    arrived_pages, arrived_slots = (
        lax.all_to_all(outgoing_pages, "seq", split_axis=1, concat_axis=1, tiled=True),
        lax.all_to_all(outgoing_slots, "seq", split_axis=1, concat_axis=1, tiled=True),
    )
    ordered_kv = jnp.concatenate(
        [every_kv[:, :ctx_count].reshape(-1, 2 * kv_width), every_kv[:, ctx_count:].reshape(-1, 2 * kv_width)],
        axis=0,
    )
    length = ordered_kv.shape[0]
    seen = (query_req[:, None] == key_req[None, :]) & (key_pos[None, :] <= query_pos[:, None])
    live = jnp.any(jnp.any(seen, axis=0).reshape(length // KEY_BLOCK, KEY_BLOCK), axis=1).astype(jnp.int32)
    rows = group * tok_count
    qreq_rows = jnp.broadcast_to(query_req[None, :], (group, tok_count)).reshape(rows, 1)
    qpos_rows = jnp.broadcast_to(query_pos[None, :], (group, tok_count)).reshape(rows, 1)
    heads_out = []
    for h in range(kv_local):
        heads_out.append(
            flash_attention(
                live,
                qreq_rows,
                qpos_rows,
                key_req.reshape(1, length),
                key_pos.reshape(1, length),
                queries[h].reshape(rows, head_dim),
                ordered_kv[:, h * head_dim:(h + 1) * head_dim],
                ordered_kv[:, kv_width + h * head_dim:kv_width + (h + 1) * head_dim],
                scale,
            ).reshape(group, tok_count, head_dim)
        )
    attn = (
        jnp.stack(heads_out, axis=0)
        .transpose(2, 0, 1, 3)
        .reshape(tok_count, query_heads * head_dim)
    )
    half = tok_count // lax.axis_size("tp")
    proj = lax.psum_scatter(
        jnp.dot(attn, w_out, preferred_element_type=jnp.float32).astype(jnp.bfloat16),
        "tp",
        scatter_dimension=0,
        tiled=True,
    ).astype(jnp.float32)
    own_rows = lax.dynamic_slice_in_dim(tokens, lax.axis_index("tp") * half, half, 0)
    resid = (own_rows.astype(jnp.float32) + proj).astype(jnp.bfloat16)
    mixed = rms_norm(resid.astype(jnp.float32), post_gain).astype(jnp.bfloat16)
    top = route_ids.shape[2]
    row_ids = route_ids[0].reshape(-1)
    row_count = row_ids.shape[0]
    seq_tp = lax.axis_size("seq") * lax.axis_size("tp")
    pd_count = lax.axis_size("pd")
    device_count = seq_tp * pd_count
    exp_local = w_gate_up.shape[0]
    experts = device_count * exp_local
    capacity = max(2, 3 * tok_count * top // (2 * lax.axis_size("tp") * experts))
    picks = (row_ids[:, None] == jnp.arange(experts, dtype=jnp.int32)[None, :]).astype(jnp.bfloat16)
    earlier = (
        lax.broadcasted_iota(jnp.int32, (row_count, row_count), 0)
        > lax.broadcasted_iota(jnp.int32, (row_count, row_count), 1)
    ).astype(jnp.bfloat16)
    before = jnp.dot(earlier, picks, preferred_element_type=jnp.float32)
    rank = jnp.sum(before * picks.astype(jnp.float32), axis=1).astype(jnp.int32)
    target = row_ids * capacity + rank
    row_token = jnp.arange(row_count, dtype=jnp.int32) // top
    lanes = 128
    chunks = width // lanes
    moe_axes = ("seq", "tp", "pd")
    slot_of = (
        target.reshape(half, top)[None, :, :]
        == jnp.arange(experts * capacity, dtype=jnp.int32)[:, None, None]
    )
    placing_rows = jnp.any(slot_of, axis=2).astype(jnp.bfloat16)
    outgoing = jnp.dot(placing_rows, mixed, preferred_element_type=jnp.float32).astype(jnp.bfloat16)
    outgoing = outgoing.reshape(device_count, exp_local * capacity * chunks, lanes)
    outgoing, arrived_pages, arrived_slots = lax.optimization_barrier(
        (outgoing, arrived_pages, arrived_slots)
    )
    arrived = lax.all_to_all(outgoing, moe_axes, split_axis=0, concat_axis=0, tiled=True)
    done = expert_mlp(arrived.reshape(device_count, exp_local, capacity, width), w_gate_up, w_down)
    returned = lax.all_to_all(
        done.reshape(device_count, exp_local * capacity * chunks, lanes),
        moe_axes,
        split_axis=0,
        concat_axis=0,
        tiled=True,
    )
    gathered = returned.reshape(experts * capacity, chunks, lanes)[target]
    weights = route_weights[0]
    weights = weights / jnp.sum(weights, axis=-1, keepdims=True)
    moe = jnp.einsum(
        "tkcl,tk->tcl",
        gathered.reshape(half, top, chunks, lanes),
        weights,
        preferred_element_type=jnp.float32,
    ).reshape(half, width)
    layer_out = (resid.astype(jnp.float32) + moe).astype(jnp.bfloat16)[None]
    placing = (arrived_slots[:, None, :] == order[None, :, None]).astype(jnp.bfloat16)
    cache = jnp.einsum(
        "hkr,hrpc->hkpc", placing, arrived_pages, preferred_element_type=jnp.float32
    ).astype(jnp.bfloat16)
    decode_cache = cache[None, :, None]
    return (layer_out, decode_cache)


def solution(mesh):
    in_specs = (
        P("pd", "seq", None),
        P(),
        P(None, "tp"),
        P(None, "tp"),
        P(None, "tp"),
        P(),
        P(),
        P("tp", None),
        P(),
        P("pd", "seq", "tp"),
        P("pd", "seq", "tp"),
        P("pd", None),
        P("pd", None),
        P("pd", ("seq", "tp"), None),
        P("pd", ("seq", "tp"), None),
        P(("seq", "tp", "pd"), None, None),
        P(("seq", "tp", "pd"), None, None),
        P(None, "pd", "seq", "tp", None),
        P(None, "pd", "seq", "tp"),
    )
    out_specs = (P("pd", ("seq", "tp"), None), P("seq", "tp", "pd", None, None, None))
    return jax.shard_map(shards, mesh=mesh, in_specs=in_specs, out_specs=out_specs, check_vma=False)
```

```python
import functools
import math

import jax
import jax.numpy as jnp
from jax import lax
from jax.experimental import pallas as pl
from jax.experimental.pallas import tpu as pltpu
from jax.sharding import PartitionSpec as P

PAGE = 128


def rms_norm(values, gain):
    return values * lax.rsqrt(jnp.mean(values * values, axis=-1, keepdims=True) + 1e-06) * gain


def rotate(values, places):
    half = values.shape[-1] // 2
    freq = jnp.exp(
        jnp.arange(half, dtype=jnp.float32) * (-2.0 * math.log(1000000.0) / values.shape[-1])
    )
    angle = places.astype(jnp.float32)[:, None] * freq[None, :]
    cosine = jnp.cos(angle)[:, None, :]
    sine = jnp.sin(angle)[:, None, :]
    first = values[..., :half]
    second = values[..., half:]
    return jnp.concatenate(
        [first * cosine - second * sine, second * cosine + first * sine], axis=-1
    )


def query_places(lengths, context_lengths, places):
    ends = jnp.cumsum(lengths)
    starts = ends - lengths
    request = jnp.sum((places[:, None] >= ends[None, :]).astype(jnp.int32), axis=1)
    member = request[:, None] == jnp.arange(lengths.shape[0], dtype=jnp.int32)[None, :]
    first = jnp.sum(jnp.where(member, starts[None, :], 0), axis=1)
    prior = jnp.sum(jnp.where(member, context_lengths[None, :], 0), axis=1)
    return (request, places - first + prior)


def context_places(context_lengths, places):
    ends = jnp.cumsum(context_lengths)
    starts = ends - context_lengths
    request = jnp.sum((places[:, None] >= ends[None, :]).astype(jnp.int32), axis=1)
    member = request[:, None] == jnp.arange(context_lengths.shape[0], dtype=jnp.int32)[None, :]
    first = jnp.sum(jnp.where(member, starts[None, :], 0), axis=1)
    return (request, places - first)


KEY_BLOCK = 512


def flash_kernel(nkb, scale, live_ref, qreq_ref, qpos_ref, kreq_ref, kpos_ref, q_ref, k_ref, v_ref, o_ref, m_sc, l_sc, acc_sc):
    kb = pl.program_id(0)

    @pl.when(kb == 0)
    def _():
        m_sc[...] = jnp.full(m_sc.shape, -1e30, jnp.float32)
        l_sc[...] = jnp.zeros(l_sc.shape, jnp.float32)
        acc_sc[...] = jnp.zeros(acc_sc.shape, jnp.float32)

    @pl.when(live_ref[kb] > 0)
    def _():
        scores = lax.dot_general(
            q_ref[...], k_ref[...], (((1,), (1,)), ((), ())), preferred_element_type=jnp.float32
        ) * scale
        visible = (qreq_ref[...] == kreq_ref[...]) & (kpos_ref[...] <= qpos_ref[...])
        heads = scores.shape[0] // visible.shape[0]
        scores = jnp.where(
            visible[None], scores.reshape((heads,) + visible.shape), -jnp.inf
        ).reshape(scores.shape)
        m_old = m_sc[...]
        m_new = jnp.maximum(m_old, jnp.max(scores, axis=1, keepdims=True))
        expo = jnp.exp(scores - m_new)
        factor = jnp.exp(m_old - m_new)
        l_sc[...] = factor * l_sc[...] + jnp.sum(expo, axis=1, keepdims=True)
        acc_sc[...] = factor * acc_sc[...] + jnp.dot(
            expo.astype(jnp.bfloat16), v_ref[...], preferred_element_type=jnp.float32
        )
        m_sc[...] = m_new

    @pl.when(kb == nkb - 1)
    def _():
        o_ref[...] = (acc_sc[...] / l_sc[...]).astype(o_ref.dtype)


def flash_attention(live, qreq, qpos, kreq, kpos, q, k, v, scale):
    rows, head_dim = q.shape
    length = k.shape[0]
    nkb = length // KEY_BLOCK
    grid_spec = pltpu.PrefetchScalarGridSpec(
        num_scalar_prefetch=1,
        grid=(nkb,),
        in_specs=[
            pl.BlockSpec(qreq.shape, lambda kb, live: (0, 0)),
            pl.BlockSpec(qpos.shape, lambda kb, live: (0, 0)),
            pl.BlockSpec((1, KEY_BLOCK), lambda kb, live: (0, kb)),
            pl.BlockSpec((1, KEY_BLOCK), lambda kb, live: (0, kb)),
            pl.BlockSpec((rows, head_dim), lambda kb, live: (0, 0)),
            pl.BlockSpec((KEY_BLOCK, head_dim), lambda kb, live: (kb, 0)),
            pl.BlockSpec((KEY_BLOCK, head_dim), lambda kb, live: (kb, 0)),
        ],
        out_specs=pl.BlockSpec((rows, head_dim), lambda kb, live: (0, 0)),
        scratch_shapes=[
            pltpu.VMEM((rows, 1), jnp.float32),
            pltpu.VMEM((rows, 1), jnp.float32),
            pltpu.VMEM((rows, head_dim), jnp.float32),
        ],
    )
    flops = 4 * rows * length * head_dim
    return pl.pallas_call(
        functools.partial(flash_kernel, nkb, scale),
        grid_spec=grid_spec,
        out_shape=jax.ShapeDtypeStruct((rows, head_dim), jnp.bfloat16),
        compiler_params=pltpu.CompilerParams(dimension_semantics=("arbitrary",)),
        cost_estimate=pl.CostEstimate(
            flops=flops, transcendentals=rows * length, bytes_accessed=2 * length * head_dim * 2 + 2 * rows * head_dim * 2
        ),
    )(live, qreq, qpos, kreq, kpos, q, k, v)


def expert_mlp(arrived, w_gate_up, w_down):
    hidden = jnp.einsum("sejd,edf->sejf", arrived, w_gate_up, preferred_element_type=jnp.float32)
    inner = hidden.shape[-1] // 2
    act = (jax.nn.silu(hidden[..., :inner]) * hidden[..., inner:]).astype(jnp.bfloat16)
    return jnp.einsum("sejf,efd->sejd", act, w_down, preferred_element_type=jnp.float32).astype(
        jnp.bfloat16
    )


def shards(
    hidden_in,
    input_gain,
    w_query,
    w_key,
    w_value,
    q_gain,
    k_gain,
    w_out,
    post_gain,
    ctx_key,
    ctx_value,
    span_lens,
    ctx_lens,
    route_ids,
    route_weights,
    w_gate_up,
    w_down,
    earlier_kv,
    page_table,
):
    tokens = hidden_in[0]
    tok_count = tokens.shape[0]
    width = tokens.shape[1]
    ctx_count = ctx_key.shape[1]
    head_dim = q_gain.shape[0]
    seq_index = lax.axis_index("seq")
    span_places = seq_index * tok_count + jnp.arange(tok_count, dtype=jnp.int32)
    ctx_index = seq_index * ctx_count + jnp.arange(ctx_count, dtype=jnp.int32)
    query_req, query_pos = query_places(span_lens[0], ctx_lens[0], span_places)
    ctx_req, ctx_pos = context_places(ctx_lens[0], ctx_index)
    normed = rms_norm(tokens.astype(jnp.float32), input_gain).astype(jnp.bfloat16)
    query = jnp.dot(normed, w_query, preferred_element_type=jnp.float32)
    key_proj = jnp.dot(normed, w_key, preferred_element_type=jnp.float32)
    value_proj = jnp.dot(normed, w_value, preferred_element_type=jnp.float32).astype(jnp.bfloat16)
    query_heads = w_query.shape[1] // head_dim
    kv_local = w_key.shape[1] // head_dim
    group = query_heads // kv_local
    queries = rotate(
        rms_norm(query.reshape(tok_count, query_heads, head_dim), q_gain), query_pos
    ).astype(jnp.bfloat16)
    queries = queries.reshape(tok_count, kv_local, group, head_dim).transpose(1, 2, 0, 3)
    span_keys = rotate(
        rms_norm(key_proj.reshape(tok_count, kv_local, head_dim), k_gain), query_pos
    ).astype(jnp.bfloat16)
    all_keys = jnp.concatenate(
        [ctx_key[0], span_keys.reshape(tok_count, kv_local * head_dim)], axis=0
    )
    all_values = jnp.concatenate([ctx_value[0], value_proj], axis=0)
    seq_size = lax.axis_size("seq")
    every_ctx_req, every_ctx_pos = context_places(
        ctx_lens[0], jnp.arange(seq_size * ctx_count, dtype=jnp.int32)
    )
    every_query_req, every_query_pos = query_places(
        span_lens[0], ctx_lens[0], jnp.arange(seq_size * tok_count, dtype=jnp.int32)
    )
    key_req = jnp.concatenate([every_ctx_req, every_query_req], axis=0)
    key_pos = jnp.concatenate([every_ctx_pos, every_query_pos], axis=0)
    scale = 1.0 / math.sqrt(head_dim)
    kv_width = kv_local * head_dim
    local_kv = jnp.concatenate([all_keys, all_values], axis=1)
    every_kv = lax.all_to_all(
        jnp.broadcast_to(local_kv[None], (seq_size,) + local_kv.shape),
        "seq",
        split_axis=0,
        concat_axis=0,
        tiled=True,
    )
    layers = earlier_kv.shape[0]
    per_device = tok_count // PAGE
    page_count = layers * per_device
    page_cap = max(1, page_count // seq_size)
    pages = earlier_kv[:, 0].reshape(layers, per_device, PAGE, kv_local, 2 * head_dim)
    pages = pages.transpose(3, 0, 1, 2, 4).reshape(kv_local, page_count, PAGE, 2 * head_dim)
    table = page_table[:, 0].transpose(2, 0, 1).reshape(kv_local, page_count)
    owners = table // page_count
    slots = table % page_count
    order = jnp.arange(page_count, dtype=jnp.int32)
    same = (owners[:, :, None] == owners[:, None, :]) & (
        order[None, None, :] < order[None, :, None]
    )
    page_rank = jnp.sum(same.astype(jnp.int32), axis=2)
    page_target = owners * page_cap + page_rank
    head_rows = jnp.broadcast_to(jnp.arange(kv_local, dtype=jnp.int32)[:, None], page_target.shape)
    outgoing_pages = (
        jnp.zeros((kv_local, seq_size * page_cap, PAGE, 2 * head_dim), jnp.bfloat16)
        .at[head_rows, page_target]
        .set(pages)
    )
    outgoing_slots = (
        jnp.full((kv_local, seq_size * page_cap), -1, jnp.int32)
        .at[head_rows, page_target]
        .set(slots)
    )
    slot_rows = 16
    slot_block = jnp.broadcast_to(
        outgoing_slots.astype(jnp.bfloat16)[:, :, None, None],
        (kv_local, seq_size * page_cap, slot_rows, 2 * head_dim),
    )
    outgoing_pages = jnp.concatenate([outgoing_pages, slot_block], axis=2)
    outgoing_pages, every_kv = lax.optimization_barrier((outgoing_pages, every_kv))
    arrived_both = lax.all_to_all(outgoing_pages, "seq", split_axis=1, concat_axis=1, tiled=True)
    arrived_pages = arrived_both[:, :, :PAGE]
    arrived_slots = arrived_both[:, :, PAGE, 0].astype(jnp.int32)
    ordered_kv = jnp.concatenate(
        [every_kv[:, :ctx_count].reshape(-1, 2 * kv_width), every_kv[:, ctx_count:].reshape(-1, 2 * kv_width)],
        axis=0,
    )
    length = ordered_kv.shape[0]
    seen = (query_req[:, None] == key_req[None, :]) & (key_pos[None, :] <= query_pos[:, None])
    live = jnp.any(jnp.any(seen, axis=0).reshape(length // KEY_BLOCK, KEY_BLOCK), axis=1).astype(jnp.int32)
    rows = group * tok_count
    qreq_rows = query_req.reshape(tok_count, 1)
    qpos_rows = query_pos.reshape(tok_count, 1)
    heads_out = []
    for h in range(kv_local):
        heads_out.append(
            flash_attention(
                live,
                qreq_rows,
                qpos_rows,
                key_req.reshape(1, length),
                key_pos.reshape(1, length),
                queries[h].reshape(rows, head_dim),
                ordered_kv[:, h * head_dim:(h + 1) * head_dim],
                ordered_kv[:, kv_width + h * head_dim:kv_width + (h + 1) * head_dim],
                scale,
            ).reshape(group, tok_count, head_dim)
        )
    attn = (
        jnp.stack(heads_out, axis=0)
        .transpose(2, 0, 1, 3)
        .reshape(tok_count, query_heads * head_dim)
    )
    half = tok_count // lax.axis_size("tp")
    proj = lax.psum_scatter(
        jnp.dot(attn, w_out, preferred_element_type=jnp.float32).astype(jnp.bfloat16),
        "tp",
        scatter_dimension=0,
        tiled=True,
    ).astype(jnp.float32)
    own_rows = lax.dynamic_slice_in_dim(tokens, lax.axis_index("tp") * half, half, 0)
    resid = (own_rows.astype(jnp.float32) + proj).astype(jnp.bfloat16)
    mixed = rms_norm(resid.astype(jnp.float32), post_gain).astype(jnp.bfloat16)
    top = route_ids.shape[2]
    row_ids = route_ids[0].reshape(-1)
    row_count = row_ids.shape[0]
    seq_tp = lax.axis_size("seq") * lax.axis_size("tp")
    pd_count = lax.axis_size("pd")
    device_count = seq_tp * pd_count
    exp_local = w_gate_up.shape[0]
    experts = device_count * exp_local
    capacity = max(2, 3 * tok_count * top // (2 * lax.axis_size("tp") * experts))
    picks = (row_ids[:, None] == jnp.arange(experts, dtype=jnp.int32)[None, :]).astype(jnp.bfloat16)
    earlier = (
        lax.broadcasted_iota(jnp.int32, (row_count, row_count), 0)
        > lax.broadcasted_iota(jnp.int32, (row_count, row_count), 1)
    ).astype(jnp.bfloat16)
    before = jnp.dot(earlier, picks, preferred_element_type=jnp.float32)
    rank = jnp.sum(before * picks.astype(jnp.float32), axis=1).astype(jnp.int32)
    target = row_ids * capacity + rank
    row_token = jnp.arange(row_count, dtype=jnp.int32) // top
    lanes = 128
    chunks = width // lanes
    moe_axes = ("seq", "tp", "pd")
    slot_of = (
        target.reshape(half, top)[None, :, :]
        == jnp.arange(experts * capacity, dtype=jnp.int32)[:, None, None]
    )
    placing_rows = jnp.any(slot_of, axis=2).astype(jnp.bfloat16)
    outgoing = jnp.dot(placing_rows, mixed, preferred_element_type=jnp.float32).astype(jnp.bfloat16)
    outgoing = outgoing.reshape(device_count, exp_local * capacity * chunks, lanes)
    outgoing, arrived_pages, arrived_slots = lax.optimization_barrier(
        (outgoing, arrived_pages, arrived_slots)
    )
    arrived = lax.all_to_all(outgoing, moe_axes, split_axis=0, concat_axis=0, tiled=True)
    done = expert_mlp(arrived.reshape(device_count, exp_local, capacity, width), w_gate_up, w_down)
    returned = lax.all_to_all(
        done.reshape(device_count, exp_local * capacity * chunks, lanes),
        moe_axes,
        split_axis=0,
        concat_axis=0,
        tiled=True,
    )
    gathered = returned.reshape(experts * capacity, chunks, lanes)[target]
    weights = route_weights[0]
    weights = weights / jnp.sum(weights, axis=-1, keepdims=True)
    moe = jnp.einsum(
        "tkcl,tk->tcl",
        gathered.reshape(half, top, chunks, lanes),
        weights,
        preferred_element_type=jnp.float32,
    ).reshape(half, width)
    layer_out = (resid.astype(jnp.float32) + moe).astype(jnp.bfloat16)[None]
    placing = (arrived_slots[:, None, :] == order[None, :, None]).astype(jnp.bfloat16)
    cache = jnp.einsum(
        "hkr,hrpc->hkpc", placing, arrived_pages, preferred_element_type=jnp.float32
    ).astype(jnp.bfloat16)
    decode_cache = cache[None, :, None]
    return (layer_out, decode_cache)


def solution(mesh):
    in_specs = (
        P("pd", "seq", None),
        P(),
        P(None, "tp"),
        P(None, "tp"),
        P(None, "tp"),
        P(),
        P(),
        P("tp", None),
        P(),
        P("pd", "seq", "tp"),
        P("pd", "seq", "tp"),
        P("pd", None),
        P("pd", None),
        P("pd", ("seq", "tp"), None),
        P("pd", ("seq", "tp"), None),
        P(("seq", "tp", "pd"), None, None),
        P(("seq", "tp", "pd"), None, None),
        P(None, "pd", "seq", "tp", None),
        P(None, "pd", "seq", "tp"),
    )
    out_specs = (P("pd", ("seq", "tp"), None), P("seq", "tp", "pd", None, None, None))
    return jax.shard_map(shards, mesh=mesh, in_specs=in_specs, out_specs=out_specs, check_vma=False)
```

```python
import functools
import math

import jax
import jax.numpy as jnp
from jax import lax
from jax.experimental import pallas as pl
from jax.experimental.pallas import tpu as pltpu
from jax.sharding import PartitionSpec as P

PAGE = 128


def rms_norm(values, gain):
    return values * lax.rsqrt(jnp.mean(values * values, axis=-1, keepdims=True) + 1e-06) * gain


def rotate(values, places):
    half = values.shape[-1] // 2
    freq = jnp.exp(
        jnp.arange(half, dtype=jnp.float32) * (-2.0 * math.log(1000000.0) / values.shape[-1])
    )
    angle = places.astype(jnp.float32)[:, None] * freq[None, :]
    cosine = jnp.cos(angle)[:, None, :]
    sine = jnp.sin(angle)[:, None, :]
    first = values[..., :half]
    second = values[..., half:]
    return jnp.concatenate(
        [first * cosine - second * sine, second * cosine + first * sine], axis=-1
    )


def query_places(lengths, context_lengths, places):
    ends = jnp.cumsum(lengths)
    starts = ends - lengths
    request = jnp.sum((places[:, None] >= ends[None, :]).astype(jnp.int32), axis=1)
    member = request[:, None] == jnp.arange(lengths.shape[0], dtype=jnp.int32)[None, :]
    first = jnp.sum(jnp.where(member, starts[None, :], 0), axis=1)
    prior = jnp.sum(jnp.where(member, context_lengths[None, :], 0), axis=1)
    return (request, places - first + prior)


def context_places(context_lengths, places):
    ends = jnp.cumsum(context_lengths)
    starts = ends - context_lengths
    request = jnp.sum((places[:, None] >= ends[None, :]).astype(jnp.int32), axis=1)
    member = request[:, None] == jnp.arange(context_lengths.shape[0], dtype=jnp.int32)[None, :]
    first = jnp.sum(jnp.where(member, starts[None, :], 0), axis=1)
    return (request, places - first)


KEY_BLOCK = 512


def flash_kernel(nkb, scale, live_ref, qreq_ref, qpos_ref, kreq_ref, kpos_ref, q_ref, k_ref, v_ref, o_ref, m_sc, l_sc, acc_sc):
    kb = pl.program_id(0)

    @pl.when(kb == 0)
    def _():
        m_sc[...] = jnp.full(m_sc.shape, -1e30, jnp.float32)
        l_sc[...] = jnp.zeros(l_sc.shape, jnp.float32)
        acc_sc[...] = jnp.zeros(acc_sc.shape, jnp.float32)

    @pl.when(live_ref[kb] > 0)
    def _():
        scores = lax.dot_general(
            q_ref[...], k_ref[...], (((1,), (1,)), ((), ())), preferred_element_type=jnp.float32
        ) * scale
        visible = (qreq_ref[...] == kreq_ref[...]) & (kpos_ref[...] <= qpos_ref[...])
        scores = jnp.where(visible, scores, -jnp.inf)
        m_old = m_sc[...]
        m_new = jnp.maximum(m_old, jnp.max(scores, axis=1, keepdims=True))
        expo = jnp.exp(scores - m_new)
        factor = jnp.exp(m_old - m_new)
        l_sc[...] = factor * l_sc[...] + jnp.sum(expo, axis=1, keepdims=True)
        acc_sc[...] = factor * acc_sc[...] + jnp.dot(
            expo.astype(jnp.bfloat16), v_ref[...], preferred_element_type=jnp.float32
        )
        m_sc[...] = m_new

    @pl.when(kb == nkb - 1)
    def _():
        o_ref[...] = (acc_sc[...] / l_sc[...]).astype(o_ref.dtype)


def flash_attention(live, qreq, qpos, kreq, kpos, q, k, v, scale):
    rows, head_dim = q.shape
    length = k.shape[0]
    nkb = length // KEY_BLOCK
    grid_spec = pltpu.PrefetchScalarGridSpec(
        num_scalar_prefetch=1,
        grid=(nkb,),
        in_specs=[
            pl.BlockSpec(qreq.shape, lambda kb, live: (0, 0)),
            pl.BlockSpec(qpos.shape, lambda kb, live: (0, 0)),
            pl.BlockSpec((1, KEY_BLOCK), lambda kb, live: (0, kb)),
            pl.BlockSpec((1, KEY_BLOCK), lambda kb, live: (0, kb)),
            pl.BlockSpec((rows, head_dim), lambda kb, live: (0, 0)),
            pl.BlockSpec((KEY_BLOCK, head_dim), lambda kb, live: (kb, 0)),
            pl.BlockSpec((KEY_BLOCK, head_dim), lambda kb, live: (kb, 0)),
        ],
        out_specs=pl.BlockSpec((rows, head_dim), lambda kb, live: (0, 0)),
        scratch_shapes=[
            pltpu.VMEM((rows, 1), jnp.float32),
            pltpu.VMEM((rows, 1), jnp.float32),
            pltpu.VMEM((rows, head_dim), jnp.float32),
        ],
    )
    flops = 4 * rows * length * head_dim
    return pl.pallas_call(
        functools.partial(flash_kernel, nkb, scale),
        grid_spec=grid_spec,
        out_shape=jax.ShapeDtypeStruct((rows, head_dim), jnp.bfloat16),
        compiler_params=pltpu.CompilerParams(dimension_semantics=("arbitrary",)),
        cost_estimate=pl.CostEstimate(
            flops=flops, transcendentals=rows * length, bytes_accessed=2 * length * head_dim * 2 + 2 * rows * head_dim * 2
        ),
    )(live, qreq, qpos, kreq, kpos, q, k, v)


def expert_mlp(arrived, w_gate_up, w_down):
    hidden = jnp.einsum("erd,edf->erf", arrived, w_gate_up, preferred_element_type=jnp.float32)
    inner = hidden.shape[-1] // 2
    act = (jax.nn.silu(hidden[..., :inner]) * hidden[..., inner:]).astype(jnp.bfloat16)
    return jnp.einsum("erf,efd->erd", act, w_down, preferred_element_type=jnp.float32).astype(
        jnp.bfloat16
    )


def shards(
    hidden_in,
    input_gain,
    w_query,
    w_key,
    w_value,
    q_gain,
    k_gain,
    w_out,
    post_gain,
    ctx_key,
    ctx_value,
    span_lens,
    ctx_lens,
    route_ids,
    route_weights,
    w_gate_up,
    w_down,
    earlier_kv,
    page_table,
):
    tokens = hidden_in[0]
    tok_count = tokens.shape[0]
    width = tokens.shape[1]
    ctx_count = ctx_key.shape[1]
    head_dim = q_gain.shape[0]
    seq_index = lax.axis_index("seq")
    span_places = seq_index * tok_count + jnp.arange(tok_count, dtype=jnp.int32)
    ctx_index = seq_index * ctx_count + jnp.arange(ctx_count, dtype=jnp.int32)
    query_req, query_pos = query_places(span_lens[0], ctx_lens[0], span_places)
    ctx_req, ctx_pos = context_places(ctx_lens[0], ctx_index)
    normed = rms_norm(tokens.astype(jnp.float32), input_gain).astype(jnp.bfloat16)
    query = jnp.dot(normed, w_query, preferred_element_type=jnp.float32)
    key_proj = jnp.dot(normed, w_key, preferred_element_type=jnp.float32)
    value_proj = jnp.dot(normed, w_value, preferred_element_type=jnp.float32).astype(jnp.bfloat16)
    query_heads = w_query.shape[1] // head_dim
    kv_local = w_key.shape[1] // head_dim
    group = query_heads // kv_local
    queries = rotate(
        rms_norm(query.reshape(tok_count, query_heads, head_dim), q_gain), query_pos
    ).astype(jnp.bfloat16)
    queries = queries.reshape(tok_count, kv_local, group, head_dim).transpose(1, 2, 0, 3)
    span_keys = rotate(
        rms_norm(key_proj.reshape(tok_count, kv_local, head_dim), k_gain), query_pos
    ).astype(jnp.bfloat16)
    all_keys = jnp.concatenate(
        [ctx_key[0], span_keys.reshape(tok_count, kv_local * head_dim)], axis=0
    )
    all_values = jnp.concatenate([ctx_value[0], value_proj], axis=0)
    seq_size = lax.axis_size("seq")
    every_ctx_req, every_ctx_pos = context_places(
        ctx_lens[0], jnp.arange(seq_size * ctx_count, dtype=jnp.int32)
    )
    every_query_req, every_query_pos = query_places(
        span_lens[0], ctx_lens[0], jnp.arange(seq_size * tok_count, dtype=jnp.int32)
    )
    key_req = jnp.concatenate([every_ctx_req, every_query_req], axis=0)
    key_pos = jnp.concatenate([every_ctx_pos, every_query_pos], axis=0)
    scale = 1.0 / math.sqrt(head_dim)
    kv_width = kv_local * head_dim
    local_kv = jnp.concatenate([all_keys, all_values], axis=1)
    every_kv = lax.all_to_all(
        jnp.broadcast_to(local_kv[None], (seq_size,) + local_kv.shape),
        "seq",
        split_axis=0,
        concat_axis=0,
        tiled=True,
    )
    layers = earlier_kv.shape[0]
    per_device = tok_count // PAGE
    page_count = layers * per_device
    page_cap = max(1, page_count // seq_size)
    pages = earlier_kv[:, 0].reshape(layers, per_device, PAGE, kv_local, 2 * head_dim)
    pages = pages.transpose(3, 0, 1, 2, 4).reshape(kv_local, page_count, PAGE, 2 * head_dim)
    table = page_table[:, 0].transpose(2, 0, 1).reshape(kv_local, page_count)
    owners = table // page_count
    slots = table % page_count
    order = jnp.arange(page_count, dtype=jnp.int32)
    same = (owners[:, :, None] == owners[:, None, :]) & (
        order[None, None, :] < order[None, :, None]
    )
    page_rank = jnp.sum(same.astype(jnp.int32), axis=2)
    page_target = owners * page_cap + page_rank
    head_rows = jnp.broadcast_to(jnp.arange(kv_local, dtype=jnp.int32)[:, None], page_target.shape)
    outgoing_pages = (
        jnp.zeros((kv_local, seq_size * page_cap, PAGE, 2 * head_dim), jnp.bfloat16)
        .at[head_rows, page_target]
        .set(pages)
    )
    outgoing_slots = (
        jnp.full((kv_local, seq_size * page_cap), -1, jnp.int32)
        .at[head_rows, page_target]
        .set(slots)
    )
    slot_rows = 16
    slot_block = jnp.broadcast_to(
        outgoing_slots.astype(jnp.bfloat16)[:, :, None, None],
        (kv_local, seq_size * page_cap, slot_rows, 2 * head_dim),
    )
    outgoing_pages = jnp.concatenate([outgoing_pages, slot_block], axis=2)
    outgoing_pages, every_kv = lax.optimization_barrier((outgoing_pages, every_kv))
    arrived_both = lax.all_to_all(outgoing_pages, "seq", split_axis=1, concat_axis=1, tiled=True)
    arrived_pages = arrived_both[:, :, :PAGE]
    arrived_slots = arrived_both[:, :, PAGE, 0].astype(jnp.int32)
    ordered_kv = jnp.concatenate(
        [every_kv[:, :ctx_count].reshape(-1, 2 * kv_width), every_kv[:, ctx_count:].reshape(-1, 2 * kv_width)],
        axis=0,
    )
    length = ordered_kv.shape[0]
    seen = (query_req[:, None] == key_req[None, :]) & (key_pos[None, :] <= query_pos[:, None])
    live = jnp.any(jnp.any(seen, axis=0).reshape(length // KEY_BLOCK, KEY_BLOCK), axis=1).astype(jnp.int32)
    rows = group * tok_count
    qreq_rows = jnp.broadcast_to(query_req[None, :], (group, tok_count)).reshape(rows, 1)
    qpos_rows = jnp.broadcast_to(query_pos[None, :], (group, tok_count)).reshape(rows, 1)
    heads_out = []
    for h in range(kv_local):
        heads_out.append(
            flash_attention(
                live,
                qreq_rows,
                qpos_rows,
                key_req.reshape(1, length),
                key_pos.reshape(1, length),
                queries[h].reshape(rows, head_dim),
                ordered_kv[:, h * head_dim:(h + 1) * head_dim],
                ordered_kv[:, kv_width + h * head_dim:kv_width + (h + 1) * head_dim],
                scale,
            ).reshape(group, tok_count, head_dim)
        )
    attn = (
        jnp.stack(heads_out, axis=0)
        .transpose(2, 0, 1, 3)
        .reshape(tok_count, query_heads * head_dim)
    )
    half = tok_count // lax.axis_size("tp")
    proj = lax.psum_scatter(
        jnp.dot(attn, w_out, preferred_element_type=jnp.float32).astype(jnp.bfloat16),
        "tp",
        scatter_dimension=0,
        tiled=True,
    ).astype(jnp.float32)
    own_rows = lax.dynamic_slice_in_dim(tokens, lax.axis_index("tp") * half, half, 0)
    resid = (own_rows.astype(jnp.float32) + proj).astype(jnp.bfloat16)
    mixed = rms_norm(resid.astype(jnp.float32), post_gain).astype(jnp.bfloat16)
    top = route_ids.shape[2]
    row_ids = route_ids[0].reshape(-1)
    row_count = row_ids.shape[0]
    seq_tp = lax.axis_size("seq") * lax.axis_size("tp")
    pd_count = lax.axis_size("pd")
    device_count = seq_tp * pd_count
    exp_local = w_gate_up.shape[0]
    experts = device_count * exp_local
    capacity = max(2, 3 * tok_count * top // (2 * lax.axis_size("tp") * experts))
    picks = (row_ids[:, None] == jnp.arange(experts, dtype=jnp.int32)[None, :]).astype(jnp.bfloat16)
    earlier = (
        lax.broadcasted_iota(jnp.int32, (row_count, row_count), 0)
        > lax.broadcasted_iota(jnp.int32, (row_count, row_count), 1)
    ).astype(jnp.bfloat16)
    before = jnp.dot(earlier, picks, preferred_element_type=jnp.float32)
    rank = jnp.sum(before * picks.astype(jnp.float32), axis=1).astype(jnp.int32)
    target = row_ids * capacity + rank
    row_token = jnp.arange(row_count, dtype=jnp.int32) // top
    lanes = 128
    chunks = width // lanes
    moe_axes = ("seq", "tp", "pd")
    slot_of = (
        target.reshape(half, top)[None, :, :]
        == jnp.arange(experts * capacity, dtype=jnp.int32)[:, None, None]
    )
    placing_rows = jnp.any(slot_of, axis=2).astype(jnp.bfloat16)
    outgoing = jnp.dot(placing_rows, mixed, preferred_element_type=jnp.float32).astype(jnp.bfloat16)
    outgoing = outgoing.reshape(device_count, exp_local * capacity * chunks, lanes)
    outgoing, arrived_pages, arrived_slots = lax.optimization_barrier(
        (outgoing, arrived_pages, arrived_slots)
    )
    arrived = lax.all_to_all(outgoing, moe_axes, split_axis=0, concat_axis=0, tiled=True)
    expert_rows = (
        arrived.reshape(device_count, exp_local, capacity, width)
        .transpose(1, 0, 2, 3)
        .reshape(exp_local, device_count * capacity, width)
    )
    done = expert_mlp(expert_rows, w_gate_up, w_down)
    done = (
        done.reshape(exp_local, device_count, capacity, width)
        .transpose(1, 0, 2, 3)
    )
    returned = lax.all_to_all(
        done.reshape(device_count, exp_local * capacity * chunks, lanes),
        moe_axes,
        split_axis=0,
        concat_axis=0,
        tiled=True,
    )
    gathered = returned.reshape(experts * capacity, chunks, lanes)[target]
    weights = route_weights[0]
    weights = weights / jnp.sum(weights, axis=-1, keepdims=True)
    moe = jnp.einsum(
        "tkcl,tk->tcl",
        gathered.reshape(half, top, chunks, lanes),
        weights,
        preferred_element_type=jnp.float32,
    ).reshape(half, width)
    layer_out = (resid.astype(jnp.float32) + moe).astype(jnp.bfloat16)[None]
    placing = (arrived_slots[:, None, :] == order[None, :, None]).astype(jnp.bfloat16)
    cache = jnp.einsum(
        "hkr,hrpc->hkpc", placing, arrived_pages, preferred_element_type=jnp.float32
    ).astype(jnp.bfloat16)
    decode_cache = cache[None, :, None]
    return (layer_out, decode_cache)


def solution(mesh):
    in_specs = (
        P("pd", "seq", None),
        P(),
        P(None, "tp"),
        P(None, "tp"),
        P(None, "tp"),
        P(),
        P(),
        P("tp", None),
        P(),
        P("pd", "seq", "tp"),
        P("pd", "seq", "tp"),
        P("pd", None),
        P("pd", None),
        P("pd", ("seq", "tp"), None),
        P("pd", ("seq", "tp"), None),
        P(("seq", "tp", "pd"), None, None),
        P(("seq", "tp", "pd"), None, None),
        P(None, "pd", "seq", "tp", None),
        P(None, "pd", "seq", "tp"),
    )
    out_specs = (P("pd", ("seq", "tp"), None), P("seq", "tp", "pd", None, None, None))
    return jax.shard_map(shards, mesh=mesh, in_specs=in_specs, out_specs=out_specs, check_vma=False)
```

```python
import functools
import math

import jax
import jax.numpy as jnp
from jax import lax
from jax.experimental import pallas as pl
from jax.experimental.pallas import tpu as pltpu
from jax.sharding import PartitionSpec as P

PAGE = 128


def rms_norm(values, gain):
    return values * lax.rsqrt(jnp.mean(values * values, axis=-1, keepdims=True) + 1e-06) * gain


def rotate(values, places):
    half = values.shape[-1] // 2
    freq = jnp.exp(
        jnp.arange(half, dtype=jnp.float32) * (-2.0 * math.log(1000000.0) / values.shape[-1])
    )
    angle = places.astype(jnp.float32)[:, None] * freq[None, :]
    cosine = jnp.cos(angle)[:, None, :]
    sine = jnp.sin(angle)[:, None, :]
    first = values[..., :half]
    second = values[..., half:]
    return jnp.concatenate(
        [first * cosine - second * sine, second * cosine + first * sine], axis=-1
    )


def query_places(lengths, context_lengths, places):
    ends = jnp.cumsum(lengths)
    starts = ends - lengths
    request = jnp.sum((places[:, None] >= ends[None, :]).astype(jnp.int32), axis=1)
    member = request[:, None] == jnp.arange(lengths.shape[0], dtype=jnp.int32)[None, :]
    first = jnp.sum(jnp.where(member, starts[None, :], 0), axis=1)
    prior = jnp.sum(jnp.where(member, context_lengths[None, :], 0), axis=1)
    return (request, places - first + prior)


def context_places(context_lengths, places):
    ends = jnp.cumsum(context_lengths)
    starts = ends - context_lengths
    request = jnp.sum((places[:, None] >= ends[None, :]).astype(jnp.int32), axis=1)
    member = request[:, None] == jnp.arange(context_lengths.shape[0], dtype=jnp.int32)[None, :]
    first = jnp.sum(jnp.where(member, starts[None, :], 0), axis=1)
    return (request, places - first)


KEY_BLOCK = 512


def flash_kernel(nkb, scale, live_ref, qreq_ref, qpos_ref, kreq_ref, kpos_ref, q_ref, k_ref, v_ref, o_ref, m_sc, l_sc, acc_sc):
    kb = pl.program_id(0)

    @pl.when(kb == 0)
    def _():
        m_sc[...] = jnp.full(m_sc.shape, -1e30, jnp.float32)
        l_sc[...] = jnp.zeros(l_sc.shape, jnp.float32)
        acc_sc[...] = jnp.zeros(acc_sc.shape, jnp.float32)

    def accumulate(masked):
        scores = lax.dot_general(
            q_ref[...], k_ref[...], (((1,), (1,)), ((), ())), preferred_element_type=jnp.float32
        ) * scale
        if masked:
            visible = (qreq_ref[...] == kreq_ref[...]) & (kpos_ref[...] <= qpos_ref[...])
            scores = jnp.where(visible, scores, -jnp.inf)
        m_old = m_sc[...]
        m_new = jnp.maximum(m_old, jnp.max(scores, axis=1, keepdims=True))
        expo = jnp.exp(scores - m_new)
        factor = jnp.exp(m_old - m_new)
        l_sc[...] = factor * l_sc[...] + jnp.sum(expo, axis=1, keepdims=True)
        acc_sc[...] = factor * acc_sc[...] + jnp.dot(
            expo.astype(jnp.bfloat16), v_ref[...], preferred_element_type=jnp.float32
        )
        m_sc[...] = m_new

    @pl.when(live_ref[kb] == 1)
    def _():
        accumulate(True)

    @pl.when(live_ref[kb] == 2)
    def _():
        accumulate(False)

    @pl.when(kb == nkb - 1)
    def _():
        o_ref[...] = (acc_sc[...] / l_sc[...]).astype(o_ref.dtype)


def flash_attention(live, qreq, qpos, kreq, kpos, q, k, v, scale):
    rows, head_dim = q.shape
    length = k.shape[0]
    nkb = length // KEY_BLOCK
    grid_spec = pltpu.PrefetchScalarGridSpec(
        num_scalar_prefetch=1,
        grid=(nkb,),
        in_specs=[
            pl.BlockSpec(qreq.shape, lambda kb, live: (0, 0)),
            pl.BlockSpec(qpos.shape, lambda kb, live: (0, 0)),
            pl.BlockSpec((1, KEY_BLOCK), lambda kb, live: (0, kb)),
            pl.BlockSpec((1, KEY_BLOCK), lambda kb, live: (0, kb)),
            pl.BlockSpec((rows, head_dim), lambda kb, live: (0, 0)),
            pl.BlockSpec((KEY_BLOCK, head_dim), lambda kb, live: (kb, 0)),
            pl.BlockSpec((KEY_BLOCK, head_dim), lambda kb, live: (kb, 0)),
        ],
        out_specs=pl.BlockSpec((rows, head_dim), lambda kb, live: (0, 0)),
        scratch_shapes=[
            pltpu.VMEM((rows, 1), jnp.float32),
            pltpu.VMEM((rows, 1), jnp.float32),
            pltpu.VMEM((rows, head_dim), jnp.float32),
        ],
    )
    flops = 4 * rows * length * head_dim
    return pl.pallas_call(
        functools.partial(flash_kernel, nkb, scale),
        grid_spec=grid_spec,
        out_shape=jax.ShapeDtypeStruct((rows, head_dim), jnp.bfloat16),
        compiler_params=pltpu.CompilerParams(dimension_semantics=("arbitrary",)),
        cost_estimate=pl.CostEstimate(
            flops=flops, transcendentals=rows * length, bytes_accessed=2 * length * head_dim * 2 + 2 * rows * head_dim * 2
        ),
    )(live, qreq, qpos, kreq, kpos, q, k, v)


def expert_mlp(arrived, w_gate_up, w_down):
    hidden = jnp.einsum("erd,edf->erf", arrived, w_gate_up, preferred_element_type=jnp.float32)
    inner = hidden.shape[-1] // 2
    act = (jax.nn.silu(hidden[..., :inner]) * hidden[..., inner:]).astype(jnp.bfloat16)
    return jnp.einsum("erf,efd->erd", act, w_down, preferred_element_type=jnp.float32).astype(
        jnp.bfloat16
    )


def shards(
    hidden_in,
    input_gain,
    w_query,
    w_key,
    w_value,
    q_gain,
    k_gain,
    w_out,
    post_gain,
    ctx_key,
    ctx_value,
    span_lens,
    ctx_lens,
    route_ids,
    route_weights,
    w_gate_up,
    w_down,
    earlier_kv,
    page_table,
):
    tokens = hidden_in[0]
    tok_count = tokens.shape[0]
    width = tokens.shape[1]
    ctx_count = ctx_key.shape[1]
    head_dim = q_gain.shape[0]
    seq_index = lax.axis_index("seq")
    span_places = seq_index * tok_count + jnp.arange(tok_count, dtype=jnp.int32)
    ctx_index = seq_index * ctx_count + jnp.arange(ctx_count, dtype=jnp.int32)
    query_req, query_pos = query_places(span_lens[0], ctx_lens[0], span_places)
    ctx_req, ctx_pos = context_places(ctx_lens[0], ctx_index)
    normed = rms_norm(tokens.astype(jnp.float32), input_gain).astype(jnp.bfloat16)
    query = jnp.dot(normed, w_query, preferred_element_type=jnp.float32)
    key_proj = jnp.dot(normed, w_key, preferred_element_type=jnp.float32)
    value_proj = jnp.dot(normed, w_value, preferred_element_type=jnp.float32).astype(jnp.bfloat16)
    query_heads = w_query.shape[1] // head_dim
    kv_local = w_key.shape[1] // head_dim
    group = query_heads // kv_local
    queries = rotate(
        rms_norm(query.reshape(tok_count, query_heads, head_dim), q_gain), query_pos
    ).astype(jnp.bfloat16)
    queries = queries.reshape(tok_count, kv_local, group, head_dim).transpose(1, 2, 0, 3)
    span_keys = rotate(
        rms_norm(key_proj.reshape(tok_count, kv_local, head_dim), k_gain), query_pos
    ).astype(jnp.bfloat16)
    all_keys = jnp.concatenate(
        [ctx_key[0], span_keys.reshape(tok_count, kv_local * head_dim)], axis=0
    )
    all_values = jnp.concatenate([ctx_value[0], value_proj], axis=0)
    seq_size = lax.axis_size("seq")
    every_ctx_req, every_ctx_pos = context_places(
        ctx_lens[0], jnp.arange(seq_size * ctx_count, dtype=jnp.int32)
    )
    every_query_req, every_query_pos = query_places(
        span_lens[0], ctx_lens[0], jnp.arange(seq_size * tok_count, dtype=jnp.int32)
    )
    key_req = jnp.concatenate([every_ctx_req, every_query_req], axis=0)
    key_pos = jnp.concatenate([every_ctx_pos, every_query_pos], axis=0)
    scale = 1.0 / math.sqrt(head_dim)
    kv_width = kv_local * head_dim
    local_kv = jnp.concatenate([all_keys, all_values], axis=1)
    every_kv = lax.all_to_all(
        jnp.broadcast_to(local_kv[None], (seq_size,) + local_kv.shape),
        "seq",
        split_axis=0,
        concat_axis=0,
        tiled=True,
    )
    layers = earlier_kv.shape[0]
    per_device = tok_count // PAGE
    page_count = layers * per_device
    page_cap = max(1, page_count // seq_size)
    pages = earlier_kv[:, 0].reshape(layers, per_device, PAGE, kv_local, 2 * head_dim)
    pages = pages.transpose(3, 0, 1, 2, 4).reshape(kv_local, page_count, PAGE, 2 * head_dim)
    table = page_table[:, 0].transpose(2, 0, 1).reshape(kv_local, page_count)
    owners = table // page_count
    slots = table % page_count
    order = jnp.arange(page_count, dtype=jnp.int32)
    same = (owners[:, :, None] == owners[:, None, :]) & (
        order[None, None, :] < order[None, :, None]
    )
    page_rank = jnp.sum(same.astype(jnp.int32), axis=2)
    page_target = owners * page_cap + page_rank
    head_rows = jnp.broadcast_to(jnp.arange(kv_local, dtype=jnp.int32)[:, None], page_target.shape)
    outgoing_pages = (
        jnp.zeros((kv_local, seq_size * page_cap, PAGE, 2 * head_dim), jnp.bfloat16)
        .at[head_rows, page_target]
        .set(pages)
    )
    outgoing_slots = (
        jnp.full((kv_local, seq_size * page_cap), -1, jnp.int32)
        .at[head_rows, page_target]
        .set(slots)
    )
    slot_rows = 16
    slot_block = jnp.broadcast_to(
        outgoing_slots.astype(jnp.bfloat16)[:, :, None, None],
        (kv_local, seq_size * page_cap, slot_rows, 2 * head_dim),
    )
    outgoing_pages = jnp.concatenate([outgoing_pages, slot_block], axis=2)
    outgoing_pages, every_kv = lax.optimization_barrier((outgoing_pages, every_kv))
    arrived_both = lax.all_to_all(outgoing_pages, "seq", split_axis=1, concat_axis=1, tiled=True)
    arrived_pages = arrived_both[:, :, :PAGE]
    arrived_slots = arrived_both[:, :, PAGE, 0].astype(jnp.int32)
    ordered_kv = jnp.concatenate(
        [every_kv[:, :ctx_count].reshape(-1, 2 * kv_width), every_kv[:, ctx_count:].reshape(-1, 2 * kv_width)],
        axis=0,
    )
    length = ordered_kv.shape[0]
    seen = (query_req[:, None] == key_req[None, :]) & (key_pos[None, :] <= query_pos[:, None])
    some_seen = jnp.any(jnp.any(seen, axis=0).reshape(length // KEY_BLOCK, KEY_BLOCK), axis=1)
    all_seen = jnp.all(jnp.all(seen, axis=0).reshape(length // KEY_BLOCK, KEY_BLOCK), axis=1)
    live = jnp.where(all_seen, 2, jnp.where(some_seen, 1, 0)).astype(jnp.int32)
    rows = group * tok_count
    qreq_rows = jnp.broadcast_to(query_req[None, :], (group, tok_count)).reshape(rows, 1)
    qpos_rows = jnp.broadcast_to(query_pos[None, :], (group, tok_count)).reshape(rows, 1)
    heads_out = []
    for h in range(kv_local):
        heads_out.append(
            flash_attention(
                live,
                qreq_rows,
                qpos_rows,
                key_req.reshape(1, length),
                key_pos.reshape(1, length),
                queries[h].reshape(rows, head_dim),
                ordered_kv[:, h * head_dim:(h + 1) * head_dim],
                ordered_kv[:, kv_width + h * head_dim:kv_width + (h + 1) * head_dim],
                scale,
            ).reshape(group, tok_count, head_dim)
        )
    attn = (
        jnp.stack(heads_out, axis=0)
        .transpose(2, 0, 1, 3)
        .reshape(tok_count, query_heads * head_dim)
    )
    half = tok_count // lax.axis_size("tp")
    proj = lax.psum_scatter(
        jnp.dot(attn, w_out, preferred_element_type=jnp.float32).astype(jnp.bfloat16),
        "tp",
        scatter_dimension=0,
        tiled=True,
    ).astype(jnp.float32)
    own_rows = lax.dynamic_slice_in_dim(tokens, lax.axis_index("tp") * half, half, 0)
    resid = (own_rows.astype(jnp.float32) + proj).astype(jnp.bfloat16)
    mixed = rms_norm(resid.astype(jnp.float32), post_gain).astype(jnp.bfloat16)
    top = route_ids.shape[2]
    row_ids = route_ids[0].reshape(-1)
    row_count = row_ids.shape[0]
    seq_tp = lax.axis_size("seq") * lax.axis_size("tp")
    pd_count = lax.axis_size("pd")
    device_count = seq_tp * pd_count
    exp_local = w_gate_up.shape[0]
    experts = device_count * exp_local
    capacity = max(2, 3 * tok_count * top // (2 * lax.axis_size("tp") * experts))
    picks = (row_ids[:, None] == jnp.arange(experts, dtype=jnp.int32)[None, :]).astype(jnp.bfloat16)
    earlier = (
        lax.broadcasted_iota(jnp.int32, (row_count, row_count), 0)
        > lax.broadcasted_iota(jnp.int32, (row_count, row_count), 1)
    ).astype(jnp.bfloat16)
    before = jnp.dot(earlier, picks, preferred_element_type=jnp.float32)
    rank = jnp.sum(before * picks.astype(jnp.float32), axis=1).astype(jnp.int32)
    target = row_ids * capacity + rank
    row_token = jnp.arange(row_count, dtype=jnp.int32) // top
    lanes = 128
    chunks = width // lanes
    moe_axes = ("seq", "tp", "pd")
    slot_of = (
        target.reshape(half, top)[None, :, :]
        == jnp.arange(experts * capacity, dtype=jnp.int32)[:, None, None]
    )
    placing_rows = jnp.any(slot_of, axis=2).astype(jnp.bfloat16)
    outgoing = jnp.dot(placing_rows, mixed, preferred_element_type=jnp.float32).astype(jnp.bfloat16)
    outgoing = outgoing.reshape(device_count, exp_local * capacity * chunks, lanes)
    outgoing, arrived_pages, arrived_slots = lax.optimization_barrier(
        (outgoing, arrived_pages, arrived_slots)
    )
    arrived = lax.all_to_all(outgoing, moe_axes, split_axis=0, concat_axis=0, tiled=True)
    expert_rows = (
        arrived.reshape(device_count, exp_local, capacity, width)
        .transpose(1, 0, 2, 3)
        .reshape(exp_local, device_count * capacity, width)
    )
    done = expert_mlp(expert_rows, w_gate_up, w_down)
    done = (
        done.reshape(exp_local, device_count, capacity, width)
        .transpose(1, 0, 2, 3)
    )
    returned = lax.all_to_all(
        done.reshape(device_count, exp_local * capacity * chunks, lanes),
        moe_axes,
        split_axis=0,
        concat_axis=0,
        tiled=True,
    )
    gathered = returned.reshape(experts * capacity, chunks, lanes)[target]
    weights = route_weights[0]
    weights = weights / jnp.sum(weights, axis=-1, keepdims=True)
    moe = jnp.einsum(
        "tkcl,tk->tcl",
        gathered.reshape(half, top, chunks, lanes),
        weights,
        preferred_element_type=jnp.float32,
    ).reshape(half, width)
    layer_out = (resid.astype(jnp.float32) + moe).astype(jnp.bfloat16)[None]
    placing = (arrived_slots[:, None, :] == order[None, :, None]).astype(jnp.bfloat16)
    cache = jnp.einsum(
        "hkr,hrpc->hkpc", placing, arrived_pages, preferred_element_type=jnp.float32
    ).astype(jnp.bfloat16)
    decode_cache = cache[None, :, None]
    return (layer_out, decode_cache)


def solution(mesh):
    in_specs = (
        P("pd", "seq", None),
        P(),
        P(None, "tp"),
        P(None, "tp"),
        P(None, "tp"),
        P(),
        P(),
        P("tp", None),
        P(),
        P("pd", "seq", "tp"),
        P("pd", "seq", "tp"),
        P("pd", None),
        P("pd", None),
        P("pd", ("seq", "tp"), None),
        P("pd", ("seq", "tp"), None),
        P(("seq", "tp", "pd"), None, None),
        P(("seq", "tp", "pd"), None, None),
        P(None, "pd", "seq", "tp", None),
        P(None, "pd", "seq", "tp"),
    )
    out_specs = (P("pd", ("seq", "tp"), None), P("seq", "tp", "pd", None, None, None))
    return jax.shard_map(shards, mesh=mesh, in_specs=in_specs, out_specs=out_specs, check_vma=False)
```

```python
import functools
import math

import jax
import jax.numpy as jnp
from jax import lax
from jax.experimental import pallas as pl
from jax.experimental.pallas import tpu as pltpu
from jax.sharding import PartitionSpec as P

PAGE = 128


def rms_norm(values, gain):
    return values * lax.rsqrt(jnp.mean(values * values, axis=-1, keepdims=True) + 1e-06) * gain


def rotate(values, places):
    half = values.shape[-1] // 2
    freq = jnp.exp(
        jnp.arange(half, dtype=jnp.float32) * (-2.0 * math.log(1000000.0) / values.shape[-1])
    )
    angle = places.astype(jnp.float32)[:, None] * freq[None, :]
    cosine = jnp.cos(angle)[:, None, :]
    sine = jnp.sin(angle)[:, None, :]
    first = values[..., :half]
    second = values[..., half:]
    return jnp.concatenate(
        [first * cosine - second * sine, second * cosine + first * sine], axis=-1
    )


def query_places(lengths, context_lengths, places):
    ends = jnp.cumsum(lengths)
    starts = ends - lengths
    request = jnp.sum((places[:, None] >= ends[None, :]).astype(jnp.int32), axis=1)
    member = request[:, None] == jnp.arange(lengths.shape[0], dtype=jnp.int32)[None, :]
    first = jnp.sum(jnp.where(member, starts[None, :], 0), axis=1)
    prior = jnp.sum(jnp.where(member, context_lengths[None, :], 0), axis=1)
    return (request, places - first + prior)


def context_places(context_lengths, places):
    ends = jnp.cumsum(context_lengths)
    starts = ends - context_lengths
    request = jnp.sum((places[:, None] >= ends[None, :]).astype(jnp.int32), axis=1)
    member = request[:, None] == jnp.arange(context_lengths.shape[0], dtype=jnp.int32)[None, :]
    first = jnp.sum(jnp.where(member, starts[None, :], 0), axis=1)
    return (request, places - first)


KEY_BLOCK = 512


def flash_kernel(nkb, scale, live_ref, qreq_ref, qpos_ref, kreq_ref, kpos_ref, q_ref, k_ref, v_ref, o_ref, m_sc, l_sc, acc_sc):
    kb = pl.program_id(0)

    @pl.when(kb == 0)
    def _():
        m_sc[...] = jnp.full(m_sc.shape, -1e30, jnp.float32)
        l_sc[...] = jnp.zeros(l_sc.shape, jnp.float32)
        acc_sc[...] = jnp.zeros(acc_sc.shape, jnp.float32)

    def accumulate(masked):
        scores = lax.dot_general(
            q_ref[...], k_ref[...], (((1,), (1,)), ((), ())), preferred_element_type=jnp.float32
        )
        if masked:
            visible = (qreq_ref[...] == kreq_ref[...]) & (kpos_ref[...] <= qpos_ref[...])
            scores = jnp.where(visible, scores, -jnp.inf)
        m_old = m_sc[...]
        m_new = jnp.maximum(m_old, jnp.max(scores, axis=1, keepdims=True))
        expo = jnp.exp((scores - m_new) * scale)
        factor = jnp.exp((m_old - m_new) * scale)
        l_sc[...] = factor * l_sc[...] + jnp.sum(expo, axis=1, keepdims=True)
        acc_sc[...] = factor * acc_sc[...] + jnp.dot(
            expo.astype(jnp.bfloat16), v_ref[...], preferred_element_type=jnp.float32
        )
        m_sc[...] = m_new

    @pl.when(live_ref[kb] == 1)
    def _():
        accumulate(True)

    @pl.when(live_ref[kb] == 2)
    def _():
        accumulate(False)

    @pl.when(kb == nkb - 1)
    def _():
        o_ref[...] = (acc_sc[...] / l_sc[...]).astype(o_ref.dtype)


def flash_attention(live, qreq, qpos, kreq, kpos, q, k, v, scale):
    rows, head_dim = q.shape
    length = k.shape[0]
    nkb = length // KEY_BLOCK
    grid_spec = pltpu.PrefetchScalarGridSpec(
        num_scalar_prefetch=1,
        grid=(nkb,),
        in_specs=[
            pl.BlockSpec(qreq.shape, lambda kb, live: (0, 0)),
            pl.BlockSpec(qpos.shape, lambda kb, live: (0, 0)),
            pl.BlockSpec((1, KEY_BLOCK), lambda kb, live: (0, kb)),
            pl.BlockSpec((1, KEY_BLOCK), lambda kb, live: (0, kb)),
            pl.BlockSpec((rows, head_dim), lambda kb, live: (0, 0)),
            pl.BlockSpec((KEY_BLOCK, head_dim), lambda kb, live: (kb, 0)),
            pl.BlockSpec((KEY_BLOCK, head_dim), lambda kb, live: (kb, 0)),
        ],
        out_specs=pl.BlockSpec((rows, head_dim), lambda kb, live: (0, 0)),
        scratch_shapes=[
            pltpu.VMEM((rows, 1), jnp.float32),
            pltpu.VMEM((rows, 1), jnp.float32),
            pltpu.VMEM((rows, head_dim), jnp.float32),
        ],
    )
    flops = 4 * rows * length * head_dim
    return pl.pallas_call(
        functools.partial(flash_kernel, nkb, scale),
        grid_spec=grid_spec,
        out_shape=jax.ShapeDtypeStruct((rows, head_dim), jnp.bfloat16),
        compiler_params=pltpu.CompilerParams(dimension_semantics=("arbitrary",)),
        cost_estimate=pl.CostEstimate(
            flops=flops, transcendentals=rows * length, bytes_accessed=2 * length * head_dim * 2 + 2 * rows * head_dim * 2
        ),
    )(live, qreq, qpos, kreq, kpos, q, k, v)


def expert_mlp(arrived, w_gate_up, w_down):
    hidden = jnp.einsum("erd,edf->erf", arrived, w_gate_up, preferred_element_type=jnp.float32)
    inner = hidden.shape[-1] // 2
    act = (jax.nn.silu(hidden[..., :inner]) * hidden[..., inner:]).astype(jnp.bfloat16)
    return jnp.einsum("erf,efd->erd", act, w_down, preferred_element_type=jnp.float32).astype(
        jnp.bfloat16
    )


def shards(
    hidden_in,
    input_gain,
    w_query,
    w_key,
    w_value,
    q_gain,
    k_gain,
    w_out,
    post_gain,
    ctx_key,
    ctx_value,
    span_lens,
    ctx_lens,
    route_ids,
    route_weights,
    w_gate_up,
    w_down,
    earlier_kv,
    page_table,
):
    tokens = hidden_in[0]
    tok_count = tokens.shape[0]
    width = tokens.shape[1]
    ctx_count = ctx_key.shape[1]
    head_dim = q_gain.shape[0]
    seq_index = lax.axis_index("seq")
    span_places = seq_index * tok_count + jnp.arange(tok_count, dtype=jnp.int32)
    ctx_index = seq_index * ctx_count + jnp.arange(ctx_count, dtype=jnp.int32)
    query_req, query_pos = query_places(span_lens[0], ctx_lens[0], span_places)
    ctx_req, ctx_pos = context_places(ctx_lens[0], ctx_index)
    normed = rms_norm(tokens.astype(jnp.float32), input_gain).astype(jnp.bfloat16)
    query = jnp.dot(normed, w_query, preferred_element_type=jnp.float32)
    key_proj = jnp.dot(normed, w_key, preferred_element_type=jnp.float32)
    value_proj = jnp.dot(normed, w_value, preferred_element_type=jnp.float32).astype(jnp.bfloat16)
    query_heads = w_query.shape[1] // head_dim
    kv_local = w_key.shape[1] // head_dim
    group = query_heads // kv_local
    queries = rotate(
        rms_norm(query.reshape(tok_count, query_heads, head_dim), q_gain), query_pos
    ).astype(jnp.bfloat16)
    queries = queries.reshape(tok_count, kv_local, group, head_dim).transpose(1, 2, 0, 3)
    span_keys = rotate(
        rms_norm(key_proj.reshape(tok_count, kv_local, head_dim), k_gain), query_pos
    ).astype(jnp.bfloat16)
    all_keys = jnp.concatenate(
        [ctx_key[0], span_keys.reshape(tok_count, kv_local * head_dim)], axis=0
    )
    all_values = jnp.concatenate([ctx_value[0], value_proj], axis=0)
    seq_size = lax.axis_size("seq")
    every_ctx_req, every_ctx_pos = context_places(
        ctx_lens[0], jnp.arange(seq_size * ctx_count, dtype=jnp.int32)
    )
    every_query_req, every_query_pos = query_places(
        span_lens[0], ctx_lens[0], jnp.arange(seq_size * tok_count, dtype=jnp.int32)
    )
    key_req = jnp.concatenate([every_ctx_req, every_query_req], axis=0)
    key_pos = jnp.concatenate([every_ctx_pos, every_query_pos], axis=0)
    scale = 1.0 / math.sqrt(head_dim)
    kv_width = kv_local * head_dim
    local_kv = jnp.concatenate([all_keys, all_values], axis=1)
    every_kv = lax.all_to_all(
        jnp.broadcast_to(local_kv[None], (seq_size,) + local_kv.shape),
        "seq",
        split_axis=0,
        concat_axis=0,
        tiled=True,
    )
    layers = earlier_kv.shape[0]
    per_device = tok_count // PAGE
    page_count = layers * per_device
    page_cap = max(1, page_count // seq_size)
    pages = earlier_kv[:, 0].reshape(layers, per_device, PAGE, kv_local, 2 * head_dim)
    pages = pages.transpose(3, 0, 1, 2, 4).reshape(kv_local, page_count, PAGE, 2 * head_dim)
    table = page_table[:, 0].transpose(2, 0, 1).reshape(kv_local, page_count)
    owners = table // page_count
    slots = table % page_count
    order = jnp.arange(page_count, dtype=jnp.int32)
    same = (owners[:, :, None] == owners[:, None, :]) & (
        order[None, None, :] < order[None, :, None]
    )
    page_rank = jnp.sum(same.astype(jnp.int32), axis=2)
    page_target = owners * page_cap + page_rank
    head_rows = jnp.broadcast_to(jnp.arange(kv_local, dtype=jnp.int32)[:, None], page_target.shape)
    outgoing_pages = (
        jnp.zeros((kv_local, seq_size * page_cap, PAGE, 2 * head_dim), jnp.bfloat16)
        .at[head_rows, page_target]
        .set(pages)
    )
    outgoing_slots = (
        jnp.full((kv_local, seq_size * page_cap), -1, jnp.int32)
        .at[head_rows, page_target]
        .set(slots)
    )
    slot_rows = 16
    slot_block = jnp.broadcast_to(
        outgoing_slots.astype(jnp.bfloat16)[:, :, None, None],
        (kv_local, seq_size * page_cap, slot_rows, 2 * head_dim),
    )
    outgoing_pages = jnp.concatenate([outgoing_pages, slot_block], axis=2)
    outgoing_pages, every_kv = lax.optimization_barrier((outgoing_pages, every_kv))
    arrived_both = lax.all_to_all(outgoing_pages, "seq", split_axis=1, concat_axis=1, tiled=True)
    arrived_pages = arrived_both[:, :, :PAGE]
    arrived_slots = arrived_both[:, :, PAGE, 0].astype(jnp.int32)
    ordered_kv = jnp.concatenate(
        [every_kv[:, :ctx_count].reshape(-1, 2 * kv_width), every_kv[:, ctx_count:].reshape(-1, 2 * kv_width)],
        axis=0,
    )
    length = ordered_kv.shape[0]
    seen = (query_req[:, None] == key_req[None, :]) & (key_pos[None, :] <= query_pos[:, None])
    some_seen = jnp.any(jnp.any(seen, axis=0).reshape(length // KEY_BLOCK, KEY_BLOCK), axis=1)
    all_seen = jnp.all(jnp.all(seen, axis=0).reshape(length // KEY_BLOCK, KEY_BLOCK), axis=1)
    live = jnp.where(all_seen, 2, jnp.where(some_seen, 1, 0)).astype(jnp.int32)
    rows = group * tok_count
    qreq_rows = jnp.broadcast_to(query_req[None, :], (group, tok_count)).reshape(rows, 1)
    qpos_rows = jnp.broadcast_to(query_pos[None, :], (group, tok_count)).reshape(rows, 1)
    heads_out = []
    for h in range(kv_local):
        heads_out.append(
            flash_attention(
                live,
                qreq_rows,
                qpos_rows,
                key_req.reshape(1, length),
                key_pos.reshape(1, length),
                queries[h].reshape(rows, head_dim),
                ordered_kv[:, h * head_dim:(h + 1) * head_dim],
                ordered_kv[:, kv_width + h * head_dim:kv_width + (h + 1) * head_dim],
                scale,
            ).reshape(group, tok_count, head_dim)
        )
    attn = (
        jnp.stack(heads_out, axis=0)
        .transpose(2, 0, 1, 3)
        .reshape(tok_count, query_heads * head_dim)
    )
    half = tok_count // lax.axis_size("tp")
    proj = lax.psum_scatter(
        jnp.dot(attn, w_out, preferred_element_type=jnp.float32).astype(jnp.bfloat16),
        "tp",
        scatter_dimension=0,
        tiled=True,
    ).astype(jnp.float32)
    own_rows = lax.dynamic_slice_in_dim(tokens, lax.axis_index("tp") * half, half, 0)
    resid = (own_rows.astype(jnp.float32) + proj).astype(jnp.bfloat16)
    mixed = rms_norm(resid.astype(jnp.float32), post_gain).astype(jnp.bfloat16)
    top = route_ids.shape[2]
    row_ids = route_ids[0].reshape(-1)
    row_count = row_ids.shape[0]
    seq_tp = lax.axis_size("seq") * lax.axis_size("tp")
    pd_count = lax.axis_size("pd")
    device_count = seq_tp * pd_count
    exp_local = w_gate_up.shape[0]
    experts = device_count * exp_local
    capacity = max(2, 3 * tok_count * top // (2 * lax.axis_size("tp") * experts))
    picks = (row_ids[:, None] == jnp.arange(experts, dtype=jnp.int32)[None, :]).astype(jnp.bfloat16)
    earlier = (
        lax.broadcasted_iota(jnp.int32, (row_count, row_count), 0)
        > lax.broadcasted_iota(jnp.int32, (row_count, row_count), 1)
    ).astype(jnp.bfloat16)
    before = jnp.dot(earlier, picks, preferred_element_type=jnp.float32)
    rank = jnp.sum(before * picks.astype(jnp.float32), axis=1).astype(jnp.int32)
    target = row_ids * capacity + rank
    row_token = jnp.arange(row_count, dtype=jnp.int32) // top
    lanes = 128
    chunks = width // lanes
    moe_axes = ("seq", "tp", "pd")
    slot_of = (
        target.reshape(half, top)[None, :, :]
        == jnp.arange(experts * capacity, dtype=jnp.int32)[:, None, None]
    )
    placing_rows = jnp.any(slot_of, axis=2).astype(jnp.bfloat16)
    outgoing = jnp.dot(placing_rows, mixed, preferred_element_type=jnp.float32).astype(jnp.bfloat16)
    outgoing = outgoing.reshape(device_count, exp_local * capacity * chunks, lanes)
    outgoing, arrived_pages, arrived_slots = lax.optimization_barrier(
        (outgoing, arrived_pages, arrived_slots)
    )
    arrived = lax.all_to_all(outgoing, moe_axes, split_axis=0, concat_axis=0, tiled=True)
    expert_rows = (
        arrived.reshape(device_count, exp_local, capacity, width)
        .transpose(1, 0, 2, 3)
        .reshape(exp_local, device_count * capacity, width)
    )
    done = expert_mlp(expert_rows, w_gate_up, w_down)
    done = (
        done.reshape(exp_local, device_count, capacity, width)
        .transpose(1, 0, 2, 3)
    )
    returned = lax.all_to_all(
        done.reshape(device_count, exp_local * capacity * chunks, lanes),
        moe_axes,
        split_axis=0,
        concat_axis=0,
        tiled=True,
    )
    gathered = returned.reshape(experts * capacity, chunks, lanes)[target]
    weights = route_weights[0]
    weights = weights / jnp.sum(weights, axis=-1, keepdims=True)
    moe = jnp.einsum(
        "tkcl,tk->tcl",
        gathered.reshape(half, top, chunks, lanes),
        weights,
        preferred_element_type=jnp.float32,
    ).reshape(half, width)
    layer_out = (resid.astype(jnp.float32) + moe).astype(jnp.bfloat16)[None]
    placing = (arrived_slots[:, None, :] == order[None, :, None]).astype(jnp.bfloat16)
    cache = jnp.einsum(
        "hkr,hrpc->hkpc", placing, arrived_pages, preferred_element_type=jnp.float32
    ).astype(jnp.bfloat16)
    decode_cache = cache[None, :, None]
    return (layer_out, decode_cache)


def solution(mesh):
    in_specs = (
        P("pd", "seq", None),
        P(),
        P(None, "tp"),
        P(None, "tp"),
        P(None, "tp"),
        P(),
        P(),
        P("tp", None),
        P(),
        P("pd", "seq", "tp"),
        P("pd", "seq", "tp"),
        P("pd", None),
        P("pd", None),
        P("pd", ("seq", "tp"), None),
        P("pd", ("seq", "tp"), None),
        P(("seq", "tp", "pd"), None, None),
        P(("seq", "tp", "pd"), None, None),
        P(None, "pd", "seq", "tp", None),
        P(None, "pd", "seq", "tp"),
    )
    out_specs = (P("pd", ("seq", "tp"), None), P("seq", "tp", "pd", None, None, None))
    return jax.shard_map(shards, mesh=mesh, in_specs=in_specs, out_specs=out_specs, check_vma=False)
```

```python
import functools
import math

import jax
import jax.numpy as jnp
from jax import lax
from jax.experimental import pallas as pl
from jax.experimental.pallas import tpu as pltpu
from jax.sharding import PartitionSpec as P

PAGE = 128


def rms_norm(values, gain):
    return values * lax.rsqrt(jnp.mean(values * values, axis=-1, keepdims=True) + 1e-06) * gain


def rotate(values, places):
    half = values.shape[-1] // 2
    freq = jnp.exp(
        jnp.arange(half, dtype=jnp.float32) * (-2.0 * math.log(1000000.0) / values.shape[-1])
    )
    angle = places.astype(jnp.float32)[:, None] * freq[None, :]
    cosine = jnp.cos(angle)[:, None, :]
    sine = jnp.sin(angle)[:, None, :]
    first = values[..., :half]
    second = values[..., half:]
    return jnp.concatenate(
        [first * cosine - second * sine, second * cosine + first * sine], axis=-1
    )


def query_places(lengths, context_lengths, places):
    ends = jnp.cumsum(lengths)
    starts = ends - lengths
    request = jnp.sum((places[:, None] >= ends[None, :]).astype(jnp.int32), axis=1)
    member = request[:, None] == jnp.arange(lengths.shape[0], dtype=jnp.int32)[None, :]
    first = jnp.sum(jnp.where(member, starts[None, :], 0), axis=1)
    prior = jnp.sum(jnp.where(member, context_lengths[None, :], 0), axis=1)
    return (request, places - first + prior)


def context_places(context_lengths, places):
    ends = jnp.cumsum(context_lengths)
    starts = ends - context_lengths
    request = jnp.sum((places[:, None] >= ends[None, :]).astype(jnp.int32), axis=1)
    member = request[:, None] == jnp.arange(context_lengths.shape[0], dtype=jnp.int32)[None, :]
    first = jnp.sum(jnp.where(member, starts[None, :], 0), axis=1)
    return (request, places - first)


KEY_BLOCK = 512


def flash_kernel(nkb, scale, live_ref, qreq_ref, qpos_ref, kreq_ref, kpos_ref, q_ref, k_ref, v_ref, o_ref, m_sc, l_sc, acc_sc):
    kb = pl.program_id(0)

    @pl.when(kb == 0)
    def _():
        m_sc[...] = jnp.full(m_sc.shape, -1e30, jnp.float32)
        l_sc[...] = jnp.zeros(l_sc.shape, jnp.float32)
        acc_sc[...] = jnp.zeros(acc_sc.shape, jnp.float32)

    def accumulate(masked):
        scores = lax.dot_general(
            q_ref[...], k_ref[...], (((1,), (1,)), ((), ())), preferred_element_type=jnp.float32
        )
        if masked:
            visible = (qreq_ref[...] == kreq_ref[...]) & (kpos_ref[...] <= qpos_ref[...])
            scores = jnp.where(visible, scores, -jnp.inf)
        m_old = m_sc[...]
        m_new = jnp.maximum(m_old, jnp.max(scores, axis=1, keepdims=True))
        expo = jnp.exp((scores - m_new) * scale)
        factor = jnp.exp((m_old - m_new) * scale)
        l_sc[...] = factor * l_sc[...] + jnp.sum(expo, axis=1, keepdims=True)
        acc_sc[...] = factor * acc_sc[...] + jnp.dot(
            expo.astype(jnp.bfloat16), v_ref[...], preferred_element_type=jnp.float32
        )
        m_sc[...] = m_new

    @pl.when(live_ref[kb] == 1)
    def _():
        accumulate(True)

    @pl.when(live_ref[kb] == 2)
    def _():
        accumulate(False)

    @pl.when(kb == nkb - 1)
    def _():
        o_ref[...] = (acc_sc[...] / l_sc[...]).astype(o_ref.dtype)


def flash_attention(live, qreq, qpos, kreq, kpos, q, k, v, scale):
    rows, head_dim = q.shape
    length = k.shape[0]
    nkb = length // KEY_BLOCK
    grid_spec = pltpu.PrefetchScalarGridSpec(
        num_scalar_prefetch=1,
        grid=(nkb,),
        in_specs=[
            pl.BlockSpec(qreq.shape, lambda kb, live: (0, 0)),
            pl.BlockSpec(qpos.shape, lambda kb, live: (0, 0)),
            pl.BlockSpec((1, KEY_BLOCK), lambda kb, live: (0, kb)),
            pl.BlockSpec((1, KEY_BLOCK), lambda kb, live: (0, kb)),
            pl.BlockSpec((rows, head_dim), lambda kb, live: (0, 0)),
            pl.BlockSpec((KEY_BLOCK, head_dim), lambda kb, live: (kb, 0)),
            pl.BlockSpec((KEY_BLOCK, head_dim), lambda kb, live: (kb, 0)),
        ],
        out_specs=pl.BlockSpec((rows, head_dim), lambda kb, live: (0, 0)),
        scratch_shapes=[
            pltpu.VMEM((rows, 1), jnp.float32),
            pltpu.VMEM((rows, 1), jnp.float32),
            pltpu.VMEM((rows, head_dim), jnp.float32),
        ],
    )
    flops = 4 * rows * length * head_dim
    return pl.pallas_call(
        functools.partial(flash_kernel, nkb, scale),
        grid_spec=grid_spec,
        out_shape=jax.ShapeDtypeStruct((rows, head_dim), jnp.bfloat16),
        compiler_params=pltpu.CompilerParams(dimension_semantics=("arbitrary",)),
        cost_estimate=pl.CostEstimate(
            flops=flops, transcendentals=rows * length, bytes_accessed=2 * length * head_dim * 2 + 2 * rows * head_dim * 2
        ),
    )(live, qreq, qpos, kreq, kpos, q, k, v)


def expert_mlp(arrived, w_gate_up, w_down):
    hidden = jnp.einsum("erd,edf->erf", arrived, w_gate_up, preferred_element_type=jnp.float32)
    inner = hidden.shape[-1] // 2
    act = (jax.nn.silu(hidden[..., :inner]) * hidden[..., inner:]).astype(jnp.bfloat16)
    return jnp.einsum("erf,efd->erd", act, w_down, preferred_element_type=jnp.float32).astype(
        jnp.bfloat16
    )


def shards(
    hidden_in,
    input_gain,
    w_query,
    w_key,
    w_value,
    q_gain,
    k_gain,
    w_out,
    post_gain,
    ctx_key,
    ctx_value,
    span_lens,
    ctx_lens,
    route_ids,
    route_weights,
    w_gate_up,
    w_down,
    earlier_kv,
    page_table,
):
    tokens = hidden_in[0]
    tok_count = tokens.shape[0]
    width = tokens.shape[1]
    ctx_count = ctx_key.shape[1]
    head_dim = q_gain.shape[0]
    seq_index = lax.axis_index("seq")
    span_places = seq_index * tok_count + jnp.arange(tok_count, dtype=jnp.int32)
    ctx_index = seq_index * ctx_count + jnp.arange(ctx_count, dtype=jnp.int32)
    query_req, query_pos = query_places(span_lens[0], ctx_lens[0], span_places)
    ctx_req, ctx_pos = context_places(ctx_lens[0], ctx_index)
    normed = rms_norm(tokens.astype(jnp.float32), input_gain).astype(jnp.bfloat16)
    query = jnp.dot(normed, w_query, preferred_element_type=jnp.float32)
    key_proj = jnp.dot(normed, w_key, preferred_element_type=jnp.float32)
    value_proj = jnp.dot(normed, w_value, preferred_element_type=jnp.float32).astype(jnp.bfloat16)
    query_heads = w_query.shape[1] // head_dim
    kv_local = w_key.shape[1] // head_dim
    group = query_heads // kv_local
    queries = rotate(
        rms_norm(query.reshape(tok_count, query_heads, head_dim), q_gain), query_pos
    ).astype(jnp.bfloat16)
    queries = queries.reshape(tok_count, kv_local, group, head_dim).transpose(1, 2, 0, 3)
    span_keys = rotate(
        rms_norm(key_proj.reshape(tok_count, kv_local, head_dim), k_gain), query_pos
    ).astype(jnp.bfloat16)
    all_keys = jnp.concatenate(
        [ctx_key[0], span_keys.reshape(tok_count, kv_local * head_dim)], axis=0
    )
    all_values = jnp.concatenate([ctx_value[0], value_proj], axis=0)
    seq_size = lax.axis_size("seq")
    every_ctx_req, every_ctx_pos = context_places(
        ctx_lens[0], jnp.arange(seq_size * ctx_count, dtype=jnp.int32)
    )
    every_query_req, every_query_pos = query_places(
        span_lens[0], ctx_lens[0], jnp.arange(seq_size * tok_count, dtype=jnp.int32)
    )
    key_req = jnp.concatenate([every_ctx_req, every_query_req], axis=0)
    key_pos = jnp.concatenate([every_ctx_pos, every_query_pos], axis=0)
    scale = 1.0 / math.sqrt(head_dim)
    kv_width = kv_local * head_dim
    local_kv = jnp.concatenate([all_keys, all_values], axis=1)
    every_kv = lax.all_to_all(
        jnp.broadcast_to(local_kv[None], (seq_size,) + local_kv.shape),
        "seq",
        split_axis=0,
        concat_axis=0,
        tiled=True,
    )
    layers = earlier_kv.shape[0]
    per_device = tok_count // PAGE
    page_count = layers * per_device
    page_cap = max(1, page_count // seq_size)
    pages = earlier_kv[:, 0].reshape(layers, per_device, PAGE, kv_local, 2 * head_dim)
    pages = pages.transpose(3, 0, 1, 2, 4).reshape(kv_local, page_count, PAGE, 2 * head_dim)
    table = page_table[:, 0].transpose(2, 0, 1).reshape(kv_local, page_count)
    owners = table // page_count
    slots = table % page_count
    order = jnp.arange(page_count, dtype=jnp.int32)
    same = (owners[:, :, None] == owners[:, None, :]) & (
        order[None, None, :] < order[None, :, None]
    )
    page_rank = jnp.sum(same.astype(jnp.int32), axis=2)
    page_target = owners * page_cap + page_rank
    head_rows = jnp.broadcast_to(jnp.arange(kv_local, dtype=jnp.int32)[:, None], page_target.shape)
    outgoing_pages = (
        jnp.zeros((kv_local, seq_size * page_cap, PAGE, 2 * head_dim), jnp.bfloat16)
        .at[head_rows, page_target]
        .set(pages)
    )
    outgoing_slots = (
        jnp.full((kv_local, seq_size * page_cap), -1, jnp.int32)
        .at[head_rows, page_target]
        .set(slots)
    )
    slot_rows = 16
    slot_block = jnp.broadcast_to(
        outgoing_slots.astype(jnp.bfloat16)[:, :, None, None],
        (kv_local, seq_size * page_cap, slot_rows, 2 * head_dim),
    )
    outgoing_pages = jnp.concatenate([outgoing_pages, slot_block], axis=2)
    outgoing_pages, every_kv = lax.optimization_barrier((outgoing_pages, every_kv))
    arrived_both = lax.all_to_all(outgoing_pages, "seq", split_axis=1, concat_axis=1, tiled=True)
    arrived_pages = arrived_both[:, :, :PAGE]
    arrived_slots = arrived_both[:, :, PAGE, 0].astype(jnp.int32)
    ordered_kv = jnp.concatenate(
        [every_kv[:, :ctx_count].reshape(-1, 2 * kv_width), every_kv[:, ctx_count:].reshape(-1, 2 * kv_width)],
        axis=0,
    )
    length = ordered_kv.shape[0]
    seen = (query_req[:, None] == key_req[None, :]) & (key_pos[None, :] <= query_pos[:, None])
    some_seen = jnp.any(jnp.any(seen, axis=0).reshape(length // KEY_BLOCK, KEY_BLOCK), axis=1)
    all_seen = jnp.all(jnp.all(seen, axis=0).reshape(length // KEY_BLOCK, KEY_BLOCK), axis=1)
    live = jnp.where(all_seen, 2, jnp.where(some_seen, 1, 0)).astype(jnp.int32)
    rows = group * tok_count
    qreq_rows = jnp.broadcast_to(query_req[None, :], (group, tok_count)).reshape(rows, 1)
    qpos_rows = jnp.broadcast_to(query_pos[None, :], (group, tok_count)).reshape(rows, 1)
    heads_out = []
    for h in range(kv_local):
        heads_out.append(
            flash_attention(
                live,
                qreq_rows,
                qpos_rows,
                key_req.reshape(1, length),
                key_pos.reshape(1, length),
                queries[h].reshape(rows, head_dim),
                ordered_kv[:, h * head_dim:(h + 1) * head_dim],
                ordered_kv[:, kv_width + h * head_dim:kv_width + (h + 1) * head_dim],
                scale,
            ).reshape(group, tok_count, head_dim)
        )
    attn = (
        jnp.stack(heads_out, axis=0)
        .transpose(2, 0, 1, 3)
        .reshape(tok_count, query_heads * head_dim)
    )
    half = tok_count // lax.axis_size("tp")
    proj = lax.psum_scatter(
        jnp.dot(attn, w_out, preferred_element_type=jnp.float32).astype(jnp.bfloat16),
        "tp",
        scatter_dimension=0,
        tiled=True,
    ).astype(jnp.float32)
    own_rows = lax.dynamic_slice_in_dim(tokens, lax.axis_index("tp") * half, half, 0)
    resid = (own_rows.astype(jnp.float32) + proj).astype(jnp.bfloat16)
    mixed = rms_norm(resid.astype(jnp.float32), post_gain).astype(jnp.bfloat16)
    top = route_ids.shape[2]
    row_ids = route_ids[0].reshape(-1)
    row_count = row_ids.shape[0]
    seq_tp = lax.axis_size("seq") * lax.axis_size("tp")
    pd_count = lax.axis_size("pd")
    device_count = seq_tp * pd_count
    exp_local = w_gate_up.shape[0]
    experts = device_count * exp_local
    capacity = max(2, 3 * tok_count * top // (2 * lax.axis_size("tp") * experts))
    picks = (row_ids[:, None] == jnp.arange(experts, dtype=jnp.int32)[None, :]).astype(jnp.bfloat16)
    earlier = (
        lax.broadcasted_iota(jnp.int32, (row_count, row_count), 0)
        > lax.broadcasted_iota(jnp.int32, (row_count, row_count), 1)
    ).astype(jnp.bfloat16)
    before = jnp.dot(earlier, picks, preferred_element_type=jnp.float32)
    rank = jnp.sum(before * picks.astype(jnp.float32), axis=1).astype(jnp.int32)
    target = row_ids * capacity + rank
    row_token = jnp.arange(row_count, dtype=jnp.int32) // top
    lanes = 128
    chunks = width // lanes
    moe_axes = ("seq", "tp", "pd")
    slot_of = (
        target.reshape(half, top)[None, :, :]
        == jnp.arange(experts * capacity, dtype=jnp.int32)[:, None, None]
    )
    placing_rows = jnp.any(slot_of, axis=2).astype(jnp.bfloat16)
    outgoing = jnp.dot(placing_rows, mixed, preferred_element_type=jnp.float32).astype(jnp.bfloat16)
    outgoing = outgoing.reshape(device_count, exp_local * capacity * chunks, lanes)
    arrived = lax.all_to_all(outgoing, moe_axes, split_axis=0, concat_axis=0, tiled=True)
    expert_rows = (
        arrived.reshape(device_count, exp_local, capacity, width)
        .transpose(1, 0, 2, 3)
        .reshape(exp_local, device_count * capacity, width)
    )
    done = expert_mlp(expert_rows, w_gate_up, w_down)
    done = (
        done.reshape(exp_local, device_count, capacity, width)
        .transpose(1, 0, 2, 3)
    )
    returned = lax.all_to_all(
        done.reshape(device_count, exp_local * capacity * chunks, lanes),
        moe_axes,
        split_axis=0,
        concat_axis=0,
        tiled=True,
    )
    gathered = returned.reshape(experts * capacity, chunks, lanes)[target]
    weights = route_weights[0]
    weights = weights / jnp.sum(weights, axis=-1, keepdims=True)
    moe = jnp.einsum(
        "tkcl,tk->tcl",
        gathered.reshape(half, top, chunks, lanes),
        weights,
        preferred_element_type=jnp.float32,
    ).reshape(half, width)
    layer_out = (resid.astype(jnp.float32) + moe).astype(jnp.bfloat16)[None]
    placing = (arrived_slots[:, None, :] == order[None, :, None]).astype(jnp.bfloat16)
    cache = jnp.einsum(
        "hkr,hrpc->hkpc", placing, arrived_pages, preferred_element_type=jnp.float32
    ).astype(jnp.bfloat16)
    decode_cache = cache[None, :, None]
    return (layer_out, decode_cache)


def solution(mesh):
    in_specs = (
        P("pd", "seq", None),
        P(),
        P(None, "tp"),
        P(None, "tp"),
        P(None, "tp"),
        P(),
        P(),
        P("tp", None),
        P(),
        P("pd", "seq", "tp"),
        P("pd", "seq", "tp"),
        P("pd", None),
        P("pd", None),
        P("pd", ("seq", "tp"), None),
        P("pd", ("seq", "tp"), None),
        P(("seq", "tp", "pd"), None, None),
        P(("seq", "tp", "pd"), None, None),
        P(None, "pd", "seq", "tp", None),
        P(None, "pd", "seq", "tp"),
    )
    out_specs = (P("pd", ("seq", "tp"), None), P("seq", "tp", "pd", None, None, None))
    return jax.shard_map(shards, mesh=mesh, in_specs=in_specs, out_specs=out_specs, check_vma=False)
```

```python
import functools
import math

import jax
import jax.numpy as jnp
from jax import lax
from jax.experimental import pallas as pl
from jax.experimental.pallas import tpu as pltpu
from jax.sharding import PartitionSpec as P

PAGE = 128


def rms_norm(values, gain):
    return values * lax.rsqrt(jnp.mean(values * values, axis=-1, keepdims=True) + 1e-06) * gain


def rotate(values, places):
    half = values.shape[-1] // 2
    freq = jnp.exp(
        jnp.arange(half, dtype=jnp.float32) * (-2.0 * math.log(1000000.0) / values.shape[-1])
    )
    angle = places.astype(jnp.float32)[:, None] * freq[None, :]
    cosine = jnp.cos(angle)[:, None, :]
    sine = jnp.sin(angle)[:, None, :]
    first = values[..., :half]
    second = values[..., half:]
    return jnp.concatenate(
        [first * cosine - second * sine, second * cosine + first * sine], axis=-1
    )


def query_places(lengths, context_lengths, places):
    ends = jnp.cumsum(lengths)
    starts = ends - lengths
    request = jnp.sum((places[:, None] >= ends[None, :]).astype(jnp.int32), axis=1)
    member = request[:, None] == jnp.arange(lengths.shape[0], dtype=jnp.int32)[None, :]
    first = jnp.sum(jnp.where(member, starts[None, :], 0), axis=1)
    prior = jnp.sum(jnp.where(member, context_lengths[None, :], 0), axis=1)
    return (request, places - first + prior)


def context_places(context_lengths, places):
    ends = jnp.cumsum(context_lengths)
    starts = ends - context_lengths
    request = jnp.sum((places[:, None] >= ends[None, :]).astype(jnp.int32), axis=1)
    member = request[:, None] == jnp.arange(context_lengths.shape[0], dtype=jnp.int32)[None, :]
    first = jnp.sum(jnp.where(member, starts[None, :], 0), axis=1)
    return (request, places - first)


KEY_BLOCK = 512


def flash_kernel(nkb, scale, live_ref, qreq_ref, qpos_ref, kreq_ref, kpos_ref, q_ref, k_ref, v_ref, o_ref, m_sc, l_sc, acc_sc):
    kb = pl.program_id(0)

    @pl.when(kb == 0)
    def _():
        m_sc[...] = jnp.full(m_sc.shape, -1e30, jnp.float32)
        l_sc[...] = jnp.zeros(l_sc.shape, jnp.float32)
        acc_sc[...] = jnp.zeros(acc_sc.shape, jnp.float32)

    def accumulate(masked):
        scores = lax.dot_general(
            q_ref[...], k_ref[...], (((1,), (1,)), ((), ())), preferred_element_type=jnp.float32
        )
        if masked:
            visible = (qreq_ref[...] == kreq_ref[...]) & (kpos_ref[...] <= qpos_ref[...])
            scores = jnp.where(visible, scores, -jnp.inf)
        m_old = m_sc[...]
        m_new = jnp.maximum(m_old, jnp.max(scores, axis=1, keepdims=True))
        expo = jnp.exp((scores - m_new) * scale)
        factor = jnp.exp((m_old - m_new) * scale)
        l_sc[...] = factor * l_sc[...] + jnp.sum(expo, axis=1, keepdims=True)
        acc_sc[...] = factor * acc_sc[...] + jnp.dot(
            expo.astype(jnp.bfloat16), v_ref[...], preferred_element_type=jnp.float32
        )
        m_sc[...] = m_new

    @pl.when(live_ref[kb] == 1)
    def _():
        accumulate(True)

    @pl.when(live_ref[kb] == 2)
    def _():
        accumulate(False)

    @pl.when(kb == nkb - 1)
    def _():
        o_ref[...] = (acc_sc[...] / l_sc[...]).astype(o_ref.dtype)


def flash_attention(live, qreq, qpos, kreq, kpos, q, k, v, scale):
    rows, head_dim = q.shape
    length = k.shape[0]
    nkb = length // KEY_BLOCK
    grid_spec = pltpu.PrefetchScalarGridSpec(
        num_scalar_prefetch=1,
        grid=(nkb,),
        in_specs=[
            pl.BlockSpec(qreq.shape, lambda kb, live: (0, 0)),
            pl.BlockSpec(qpos.shape, lambda kb, live: (0, 0)),
            pl.BlockSpec((1, KEY_BLOCK), lambda kb, live: (0, kb)),
            pl.BlockSpec((1, KEY_BLOCK), lambda kb, live: (0, kb)),
            pl.BlockSpec((rows, head_dim), lambda kb, live: (0, 0)),
            pl.BlockSpec((KEY_BLOCK, head_dim), lambda kb, live: (kb, 0)),
            pl.BlockSpec((KEY_BLOCK, head_dim), lambda kb, live: (kb, 0)),
        ],
        out_specs=pl.BlockSpec((rows, head_dim), lambda kb, live: (0, 0)),
        scratch_shapes=[
            pltpu.VMEM((rows, 1), jnp.float32),
            pltpu.VMEM((rows, 1), jnp.float32),
            pltpu.VMEM((rows, head_dim), jnp.float32),
        ],
    )
    flops = 4 * rows * length * head_dim
    return pl.pallas_call(
        functools.partial(flash_kernel, nkb, scale),
        grid_spec=grid_spec,
        out_shape=jax.ShapeDtypeStruct((rows, head_dim), jnp.bfloat16),
        compiler_params=pltpu.CompilerParams(dimension_semantics=("arbitrary",)),
        cost_estimate=pl.CostEstimate(
            flops=flops, transcendentals=rows * length, bytes_accessed=2 * length * head_dim * 2 + 2 * rows * head_dim * 2
        ),
    )(live, qreq, qpos, kreq, kpos, q, k, v)


def expert_mlp(arrived, w_gate_up, w_down):
    hidden = jnp.einsum("erd,edf->erf", arrived, w_gate_up, preferred_element_type=jnp.float32)
    inner = hidden.shape[-1] // 2
    act = (jax.nn.silu(hidden[..., :inner]) * hidden[..., inner:]).astype(jnp.bfloat16)
    return jnp.einsum("erf,efd->erd", act, w_down, preferred_element_type=jnp.float32).astype(
        jnp.bfloat16
    )


def shards(
    hidden_in,
    input_gain,
    w_query,
    w_key,
    w_value,
    q_gain,
    k_gain,
    w_out,
    post_gain,
    ctx_key,
    ctx_value,
    span_lens,
    ctx_lens,
    route_ids,
    route_weights,
    w_gate_up,
    w_down,
    earlier_kv,
    page_table,
):
    tokens = hidden_in[0]
    tok_count = tokens.shape[0]
    width = tokens.shape[1]
    ctx_count = ctx_key.shape[1]
    head_dim = q_gain.shape[0]
    seq_index = lax.axis_index("seq")
    span_places = seq_index * tok_count + jnp.arange(tok_count, dtype=jnp.int32)
    ctx_index = seq_index * ctx_count + jnp.arange(ctx_count, dtype=jnp.int32)
    query_req, query_pos = query_places(span_lens[0], ctx_lens[0], span_places)
    ctx_req, ctx_pos = context_places(ctx_lens[0], ctx_index)
    normed = rms_norm(tokens.astype(jnp.float32), input_gain).astype(jnp.bfloat16)
    query = jnp.dot(normed, w_query, preferred_element_type=jnp.float32)
    key_proj = jnp.dot(normed, w_key, preferred_element_type=jnp.float32)
    value_proj = jnp.dot(normed, w_value, preferred_element_type=jnp.float32).astype(jnp.bfloat16)
    query_heads = w_query.shape[1] // head_dim
    kv_local = w_key.shape[1] // head_dim
    group = query_heads // kv_local
    queries = rotate(
        rms_norm(query.reshape(tok_count, query_heads, head_dim), q_gain), query_pos
    ).astype(jnp.bfloat16)
    queries = queries.reshape(tok_count, kv_local, group, head_dim).transpose(1, 2, 0, 3)
    span_keys = rotate(
        rms_norm(key_proj.reshape(tok_count, kv_local, head_dim), k_gain), query_pos
    ).astype(jnp.bfloat16)
    all_keys = jnp.concatenate(
        [ctx_key[0], span_keys.reshape(tok_count, kv_local * head_dim)], axis=0
    )
    all_values = jnp.concatenate([ctx_value[0], value_proj], axis=0)
    seq_size = lax.axis_size("seq")
    every_ctx_req, every_ctx_pos = context_places(
        ctx_lens[0], jnp.arange(seq_size * ctx_count, dtype=jnp.int32)
    )
    every_query_req, every_query_pos = query_places(
        span_lens[0], ctx_lens[0], jnp.arange(seq_size * tok_count, dtype=jnp.int32)
    )
    key_req = jnp.concatenate([every_ctx_req, every_query_req], axis=0)
    key_pos = jnp.concatenate([every_ctx_pos, every_query_pos], axis=0)
    scale = 1.0 / math.sqrt(head_dim)
    kv_width = kv_local * head_dim
    local_kv = jnp.concatenate([all_keys, all_values], axis=1)
    every_kv = lax.all_to_all(
        jnp.broadcast_to(local_kv[None], (seq_size,) + local_kv.shape),
        "seq",
        split_axis=0,
        concat_axis=0,
        tiled=True,
    )
    layers = earlier_kv.shape[0]
    per_device = tok_count // PAGE
    page_count = layers * per_device
    page_cap = max(1, page_count // seq_size)
    pages = earlier_kv[:, 0].reshape(layers, per_device, PAGE, kv_local, 2 * head_dim)
    pages = pages.transpose(3, 0, 1, 2, 4).reshape(kv_local, page_count, PAGE, 2 * head_dim)
    table = page_table[:, 0].transpose(2, 0, 1).reshape(kv_local, page_count)
    owners = table // page_count
    slots = table % page_count
    order = jnp.arange(page_count, dtype=jnp.int32)
    same = (owners[:, :, None] == owners[:, None, :]) & (
        order[None, None, :] < order[None, :, None]
    )
    page_rank = jnp.sum(same.astype(jnp.int32), axis=2)
    page_target = owners * page_cap + page_rank
    head_rows = jnp.broadcast_to(jnp.arange(kv_local, dtype=jnp.int32)[:, None], page_target.shape)
    outgoing_pages = (
        jnp.zeros((kv_local, seq_size * page_cap, PAGE, 2 * head_dim), jnp.bfloat16)
        .at[head_rows, page_target]
        .set(pages)
    )
    outgoing_slots = (
        jnp.full((kv_local, seq_size * page_cap), -1, jnp.int32)
        .at[head_rows, page_target]
        .set(slots)
    )
    slot_rows = 16
    slot_block = jnp.broadcast_to(
        outgoing_slots.astype(jnp.bfloat16)[:, :, None, None],
        (kv_local, seq_size * page_cap, slot_rows, 2 * head_dim),
    )
    outgoing_pages = jnp.concatenate([outgoing_pages, slot_block], axis=2)
    outgoing_pages, every_kv = lax.optimization_barrier((outgoing_pages, every_kv))
    arrived_both = lax.all_to_all(outgoing_pages, "seq", split_axis=1, concat_axis=1, tiled=True)
    arrived_pages = arrived_both[:, :, :PAGE]
    arrived_slots = arrived_both[:, :, PAGE, 0].astype(jnp.int32)
    ordered_kv = jnp.concatenate(
        [every_kv[:, :ctx_count].reshape(-1, 2 * kv_width), every_kv[:, ctx_count:].reshape(-1, 2 * kv_width)],
        axis=0,
    )
    length = ordered_kv.shape[0]
    seen = (query_req[:, None] == key_req[None, :]) & (key_pos[None, :] <= query_pos[:, None])
    some_seen = jnp.any(jnp.any(seen, axis=0).reshape(length // KEY_BLOCK, KEY_BLOCK), axis=1)
    all_seen = jnp.all(jnp.all(seen, axis=0).reshape(length // KEY_BLOCK, KEY_BLOCK), axis=1)
    live = jnp.where(all_seen, 2, jnp.where(some_seen, 1, 0)).astype(jnp.int32)
    rows = group * tok_count
    qreq_rows = jnp.broadcast_to(query_req[None, :], (group, tok_count)).reshape(rows, 1)
    qpos_rows = jnp.broadcast_to(query_pos[None, :], (group, tok_count)).reshape(rows, 1)
    heads_out = []
    for h in range(kv_local):
        heads_out.append(
            flash_attention(
                live,
                qreq_rows,
                qpos_rows,
                key_req.reshape(1, length),
                key_pos.reshape(1, length),
                queries[h].reshape(rows, head_dim),
                ordered_kv[:, h * head_dim:(h + 1) * head_dim],
                ordered_kv[:, kv_width + h * head_dim:kv_width + (h + 1) * head_dim],
                scale,
            ).reshape(group, tok_count, head_dim)
        )
    attn = (
        jnp.stack(heads_out, axis=0)
        .transpose(2, 0, 1, 3)
        .reshape(tok_count, query_heads * head_dim)
    )
    half = tok_count // lax.axis_size("tp")
    proj = lax.psum_scatter(
        jnp.dot(attn, w_out, preferred_element_type=jnp.float32).astype(jnp.bfloat16),
        "tp",
        scatter_dimension=0,
        tiled=True,
    ).astype(jnp.float32)
    own_rows = lax.dynamic_slice_in_dim(tokens, lax.axis_index("tp") * half, half, 0)
    resid = (own_rows.astype(jnp.float32) + proj).astype(jnp.bfloat16)
    mixed = rms_norm(resid.astype(jnp.float32), post_gain).astype(jnp.bfloat16)
    top = route_ids.shape[2]
    row_ids = route_ids[0].reshape(-1)
    row_count = row_ids.shape[0]
    seq_tp = lax.axis_size("seq") * lax.axis_size("tp")
    pd_count = lax.axis_size("pd")
    device_count = seq_tp * pd_count
    exp_local = w_gate_up.shape[0]
    experts = device_count * exp_local
    capacity = max(2, 3 * tok_count * top // (2 * lax.axis_size("tp") * experts))
    picks = (row_ids[:, None] == jnp.arange(experts, dtype=jnp.int32)[None, :]).astype(jnp.bfloat16)
    earlier = (
        lax.broadcasted_iota(jnp.int32, (row_count, row_count), 0)
        > lax.broadcasted_iota(jnp.int32, (row_count, row_count), 1)
    ).astype(jnp.bfloat16)
    before = jnp.dot(earlier, picks, preferred_element_type=jnp.float32)
    rank = jnp.sum(before * picks.astype(jnp.float32), axis=1).astype(jnp.int32)
    target = row_ids * capacity + rank
    row_token = jnp.arange(row_count, dtype=jnp.int32) // top
    lanes = 128
    chunks = width // lanes
    moe_axes = ("seq", "tp", "pd")
    slot_of = (
        target.reshape(half, top)[None, :, :]
        == jnp.arange(experts * capacity, dtype=jnp.int32)[:, None, None]
    )
    placing_rows = jnp.any(slot_of, axis=2).astype(jnp.bfloat16)
    outgoing = jnp.einsum(
        "st,tcl->scl", placing_rows, mixed.reshape(half, chunks, lanes), preferred_element_type=jnp.float32
    ).astype(jnp.bfloat16)
    outgoing = outgoing.reshape(device_count, exp_local * capacity * chunks, lanes)
    outgoing, arrived_pages, arrived_slots = lax.optimization_barrier(
        (outgoing, arrived_pages, arrived_slots)
    )
    arrived = lax.all_to_all(outgoing, moe_axes, split_axis=0, concat_axis=0, tiled=True)
    expert_rows = (
        arrived.reshape(device_count, exp_local, capacity, width)
        .transpose(1, 0, 2, 3)
        .reshape(exp_local, device_count * capacity, width)
    )
    done = expert_mlp(expert_rows, w_gate_up, w_down)
    done = (
        done.reshape(exp_local, device_count, capacity, width)
        .transpose(1, 0, 2, 3)
    )
    returned = lax.all_to_all(
        done.reshape(device_count, exp_local * capacity * chunks, lanes),
        moe_axes,
        split_axis=0,
        concat_axis=0,
        tiled=True,
    )
    gathered = returned.reshape(experts * capacity, chunks, lanes)[target]
    weights = route_weights[0]
    weights = weights / jnp.sum(weights, axis=-1, keepdims=True)
    moe = jnp.einsum(
        "tkcl,tk->tcl",
        gathered.reshape(half, top, chunks, lanes),
        weights,
        preferred_element_type=jnp.float32,
    ).reshape(half, width)
    layer_out = (resid.astype(jnp.float32) + moe).astype(jnp.bfloat16)[None]
    placing = (arrived_slots[:, None, :] == order[None, :, None]).astype(jnp.bfloat16)
    cache = jnp.einsum(
        "hkr,hrpc->hkpc", placing, arrived_pages, preferred_element_type=jnp.float32
    ).astype(jnp.bfloat16)
    decode_cache = cache[None, :, None]
    return (layer_out, decode_cache)


def solution(mesh):
    in_specs = (
        P("pd", "seq", None),
        P(),
        P(None, "tp"),
        P(None, "tp"),
        P(None, "tp"),
        P(),
        P(),
        P("tp", None),
        P(),
        P("pd", "seq", "tp"),
        P("pd", "seq", "tp"),
        P("pd", None),
        P("pd", None),
        P("pd", ("seq", "tp"), None),
        P("pd", ("seq", "tp"), None),
        P(("seq", "tp", "pd"), None, None),
        P(("seq", "tp", "pd"), None, None),
        P(None, "pd", "seq", "tp", None),
        P(None, "pd", "seq", "tp"),
    )
    out_specs = (P("pd", ("seq", "tp"), None), P("seq", "tp", "pd", None, None, None))
    return jax.shard_map(shards, mesh=mesh, in_specs=in_specs, out_specs=out_specs, check_vma=False)
```
